256 devices in a mesh: dp: 64 (over x, z, core), mp: 4 (over y).
Axes of the slice: x: 4, y: 4, z: 8, core: 2. Of those that a mesh axis runs over, the one named last changes fastest.
Arguments:
- attn: bfloat16 [2, 4096, 2048], P(None, 'dp', 'mp'), may hold values from -6 to 6
- resid: bfloat16 [2, 4096, 4096], P(None, 'dp', 'mp'), may hold values from -6 to 6
- w_out: bfloat16 [4096, 2048], P('dp', 'mp'), may hold values from -0.125 to 0.125
- gain: float32 [4096], P('mp'), may hold values from 0.1 to 1.9
- neg_owner: int32 [4096, 31], P('dp'), may hold values from 0 to 63, as said below
- neg_local: int32 [4096, 31], P('dp'), may hold values from 0 to 63
Outputs:
- attn_grad: bfloat16 [2, 4096, 2048], P(None, 'dp', 'mp')
- weight_grad: float32 [4096, 2048], P('dp', 'mp')
- gain_grad: float32 [4096], P('mp')
The draws below stay inside these ranges and needn't reach their ends.
Inputs may be any that keep to these rules, and one draw needn't show every extreme that they name: `neg_owner`: among the 64 queries of one index of dp (aligned blocks of rows), no owner is named more than 62 times, and some owner exactly 62 times.
All inputs are finite; a program needn't handle non-finite values.
Results may differ from the reference program's by a relative error of at most 0.0052.
Values may be sent and summed in bfloat16 or wider, within the bound.
No kernel may reach another device: no remote copies, remote signals or barrier semaphores. Data moves between devices by JAX's collectives and lax.ppermute only.
A program may use at most 128 MiB of HBM per device.

```python
import jax
import jax.numpy as jnp
from jax import lax

D = 4096
HD = 2048
NEG = 31
PAIRS_DEV = 64
PAIRS = 4096
CAP = 62
N_DP = 64


def draw_neg_owner(key, part):
    keys = jax.random.split(key, N_DP)
    total = N_DP * CAP

    def one_block(block_key):
        key_hot, key_order, key_shuffle = jax.random.split(block_key, 3)
        hot = jax.random.randint(key_hot, (), 0, N_DP)
        slots = jnp.arange(total, dtype=jnp.int32)
        owner = slots // CAP
        order = jax.random.permutation(key_order, total).astype(jnp.int32)
        position = jnp.zeros((total,), jnp.int32).at[order].set(slots)
        ranking = jnp.where(owner == hot, slots - total, position)
        chosen = jnp.argsort(ranking)[:PAIRS_DEV * NEG]
        picked = jax.random.permutation(key_shuffle, owner[chosen])
        return picked.reshape(PAIRS_DEV, NEG)
    return jax.vmap(one_block)(keys).reshape(PAIRS_DEV * N_DP, NEG).astype(jnp.int32)


def set_ends(entries, own_key, least, high):
    index_at = [jax.random.randint(jax.random.fold_in(own_key, axis), (), 0, length) for axis, length in enumerate(entries.shape)]
    longest = entries.shape.index(max(entries.shape))
    next_to = index_at[:longest] + [(index_at[longest] + 1) % entries.shape[longest]] + index_at[longest + 1:]
    return entries.at[tuple(index_at)].set(least).at[tuple(next_to)].set(high)


def shard_levels(own_key, dims, cuts, low, top_value):
    def one(axis_at, parts):
        draws = jax.random.uniform(jax.random.fold_in(jax.random.fold_in(own_key, 6), axis_at), (parts,), jnp.float32, low / len(cuts), top_value / len(cuts))
        return jnp.repeat(jnp.exp(draws), dims[axis_at] // parts).reshape((-1,) + (1,) * (len(dims) - axis_at - 1))

    loudness = one(*cuts[0])
    for cut in cuts[1:]:
        loudness = loudness * one(*cut)
    return loudness


def noise(stream_key, extent, spread, bound, pieces=(), kind=jnp.bfloat16):
    entries = jax.random.normal(stream_key, extent, jnp.float32) * spread
    if len(pieces) > 0:
        entries = shard_levels(stream_key, extent, pieces, -0.22, 0.18) * entries
    return jnp.clip(entries, min=-bound, max=bound).astype(kind)


def setup_inputs(seed: int = 0) -> dict:
    streams_of = jax.random.split(jax.random.key(seed), 7)
    attn = noise(streams_of[0], (2, PAIRS, HD), 1.0, 6.0, ((1, 64), (2, 4)))
    resid = noise(streams_of[1], (2, PAIRS, D), 1.0, 6.0, ((1, 64), (2, 4)))
    w_out = noise(streams_of[2], (D, HD), HD ** -0.5, 0.125, ((0, 64), (1, 4)))
    gain = jnp.clip(1.0 + 0.18 * jax.random.normal(streams_of[3], (D,), jnp.float32), 0.1, 1.9)
    neg_owner = draw_neg_owner(jax.random.fold_in(streams_of[6], 71), 0)
    neg_local = set_ends(jax.random.randint(streams_of[5], (PAIRS, NEG), 0, PAIRS_DEV), jax.random.fold_in(streams_of[5], 1), 0, PAIRS_DEV - 1).astype(jnp.int32)
    return dict(attn=attn, resid=resid, w_out=w_out, gain=gain, neg_owner=neg_owner, neg_local=neg_local)


TAU = 0.05
LOSS_SCALE = 32.0
EPS = 1e-06

def reference(attn, resid, w_out, gain, neg_owner, neg_local):
    rows_a = attn.reshape(2 * PAIRS, HD)
    proj = jnp.dot(rows_a, w_out.T, preferred_element_type=jnp.float32)
    hidden = resid.reshape(2 * PAIRS, D).astype(jnp.float32) + proj
    normed = hidden * gain
    recip = lax.rsqrt(lax.optimization_barrier(jnp.sum(normed * normed, axis=1, keepdims=True)) + EPS)
    emb = (normed * recip).astype(jnp.bfloat16)
    query = emb[:PAIRS].astype(jnp.float32)
    docs = emb[PAIRS:].astype(jnp.float32)
    doc_ids = (neg_owner * PAIRS_DEV + neg_local).astype(jnp.int32)
    ids_t = jnp.transpose(doc_ids)
    pos_score = lax.optimization_barrier(jnp.sum(query * docs, axis=1)) / TAU

    def neg_score(ids):
        return lax.optimization_barrier(jnp.sum(query * docs[ids], axis=1)) / TAU
    neg_scores = jnp.transpose(lax.map(neg_score, ids_t))
    scores = jnp.concatenate([pos_score[:, None], neg_scores], axis=1)
    expo = jnp.exp(scores)
    prob = expo / lax.optimization_barrier(jnp.sum(expo, axis=1, keepdims=True))
    first = (jnp.arange(NEG + 1) == 0).astype(jnp.float32)[None, :]
    wts = LOSS_SCALE * (prob - first) / TAU

    def accum(carry, inputs):
        dq_acc, dd_acc = carry
        ids, wcol = inputs
        dq_acc = dq_acc + wcol[:, None] * docs[ids]
        term = (wcol[:, None] * query).astype(jnp.bfloat16).astype(jnp.float32)
        dd_acc = dd_acc + jax.ops.segment_sum(term, ids, num_segments=PAIRS)
        return ((dq_acc, dd_acc), None)
    start = (wts[:, 0:1] * docs, wts[:, 0:1] * query)
    (dq, dd), _ = lax.scan(accum, start, (ids_t, jnp.transpose(wts[:, 1:])))
    demb = jnp.concatenate([dq, dd], axis=0)
    inner = lax.optimization_barrier(jnp.sum(normed * demb, axis=1, keepdims=True))
    dnorm = recip * demb - recip * recip * recip * normed * inner
    gain_grad = lax.optimization_barrier(jnp.sum(dnorm * hidden, axis=0))
    dh = (dnorm * gain).astype(jnp.bfloat16)
    attn_grad = jnp.dot(dh, w_out, preferred_element_type=jnp.float32).astype(jnp.bfloat16).reshape(2, PAIRS, HD)
    weight_grad = jnp.dot(dh.T, rows_a, preferred_element_type=jnp.float32)
    return (attn_grad, weight_grad, gain_grad)
```

```python
import jax
import jax.numpy as jnp
import numpy as np
from jax import lax
from jax.sharding import Mesh, PartitionSpec as P

TAU = 0.05
LOSS_SCALE = 32.0
EPS = 1e-06
XZ = ("x", "z")
DP = ("x", "z", "c")


def gather_dp(v):
    return lax.all_gather(lax.all_gather(v, XZ, axis=0, tiled=True), "c", axis=0, tiled=True)


def split_bf16(v):
    hi = v.astype(jnp.bfloat16)
    lo = (v - hi.astype(jnp.float32)).astype(jnp.bfloat16)
    return jnp.concatenate([hi, lo], axis=0)


def mm(a, b):
    return jnp.dot(a, b, preferred_element_type=jnp.float32)


def shards(attn, resid, w_out, gain, neg_owner, neg_local):
    n_xz = lax.axis_size("x") * lax.axis_size("z")
    n_c = lax.axis_size("c")
    pairs_here = attn.shape[1]
    heads = attn.shape[2]
    feats = resid.shape[2]
    w_rows = w_out.shape[0]
    total = pairs_here * n_xz * n_c

    pos = ((neg_owner % n_c) * n_xz + neg_owner // n_c) * pairs_here + neg_local
    pos_t = pos.T
    pos_all_t = gather_dp(pos).T

    w_cxz = gather_dp(w_out)
    weight_full = (
        w_cxz.reshape(n_c, n_xz, w_rows, heads).transpose(1, 0, 2, 3).reshape(-1, heads)
    )
    rows_a = attn.reshape(2 * pairs_here, heads)
    proj_part = lax.dot_general(
        rows_a, weight_full, (((1,), (1,)), ((), ())), preferred_element_type=jnp.float32
    )
    proj = lax.psum_scatter(proj_part, "mp", scatter_dimension=1, tiled=True)
    hidden = resid.reshape(2 * pairs_here, feats).astype(jnp.float32) + proj
    normed = hidden * gain
    squares = lax.psum(jnp.sum(normed * normed, axis=1), "mp")
    recip = lax.rsqrt(squares + EPS)[:, None]
    emb = (normed * recip).astype(jnp.bfloat16)
    query = emb[:pairs_here]
    docs = emb[pairs_here:]
    query_f = query.astype(jnp.float32)
    docs_f = docs.astype(jnp.float32)
    q_all = gather_dp(query)
    e_all = gather_dp(docs)

    all_scores = lax.dot_general(
        query, e_all, (((1,), (1,)), ((), ())), preferred_element_type=jnp.float32
    )
    neg_part = jnp.take_along_axis(all_scores, pos, axis=1)
    pos_part = jnp.sum(query_f * docs_f, axis=1)
    partial_value = jnp.concatenate([pos_part[:, None], neg_part], axis=1)
    scores = lax.psum(partial_value, "mp") / TAU
    expo = jnp.exp(scores)
    prob = expo / jnp.sum(expo, axis=1, keepdims=True)
    first = (jnp.arange(scores.shape[1]) == 0).astype(jnp.float32)[None, :]
    wts = LOSS_SCALE * (prob - first) / TAU
    wts_neg_t = wts[:, 1:].T
    wts_all_t = gather_dp(wts[:, 1:]).T

    cols = lax.broadcasted_iota(jnp.int32, (1, 1, total), 2)
    coef_q = jnp.sum(jnp.where(pos_t[:, :, None] == cols, wts_neg_t[:, :, None], 0.0), axis=0)
    both = mm(split_bf16(coef_q), e_all)
    grad_query = wts[:, 0:1] * docs_f + both[:pairs_here] + both[pairs_here:]

    me = lax.axis_index("c") * n_xz + lax.axis_index(XZ)
    own = me * pairs_here + lax.broadcasted_iota(jnp.int32, (1, pairs_here, 1), 1)
    coef_d = jnp.sum(jnp.where(pos_all_t[:, None, :] == own, wts_all_t[:, None, :], 0.0), axis=0)
    both_d = mm(split_bf16(coef_d), q_all)
    grad_docs = wts[:, 0:1] * query_f + both_d[:pairs_here] + both_d[pairs_here:]

    demb = jnp.concatenate([grad_query, grad_docs], axis=0)
    inner = lax.psum(jnp.sum(normed * demb, axis=1), "mp")[:, None]
    dnorm = recip * demb - recip * recip * recip * normed * inner
    gain_grad = lax.psum(jnp.sum(dnorm * hidden, axis=0), DP)
    dh = (dnorm * gain).astype(jnp.bfloat16)
    dh_full = lax.all_gather(dh, "mp", axis=1, tiled=True)
    attn_grad = mm(dh_full, weight_full).astype(jnp.bfloat16).reshape(attn.shape)
    rows = dh_full.shape[0]
    dh_perm = dh_full.reshape(rows, n_xz, n_c, w_rows).transpose(0, 2, 1, 3).reshape(rows, -1)
    wg_part = lax.dot_general(
        dh_perm, rows_a, (((0,), (0,)), ((), ())), preferred_element_type=jnp.float32
    )
    wg_c = lax.psum_scatter(wg_part, "c", scatter_dimension=0, tiled=True)
    weight_grad = lax.psum_scatter(wg_c, XZ, scatter_dimension=0, tiled=True)
    return (attn_grad, weight_grad, gain_grad)


def split_mesh(mesh):
    grid = mesh.devices
    n_dp, n_mp = grid.shape
    column = grid[:, 0]
    n_x = len({d.coords[0] for d in column})
    n_c = len({d.core_on_chip for d in column})
    n_z = n_dp // (n_x * n_c)
    return Mesh(grid.reshape(n_x, n_z, n_c, n_mp), ("x", "z", "c", "mp"))


def solution(mesh):
    inner_mesh = split_mesh(mesh)
    in_specs = (
        P(None, DP, "mp"),
        P(None, DP, "mp"),
        P(DP, "mp"),
        P("mp"),
        P(DP, None),
        P(DP, None),
    )
    out_specs = (P(None, DP, "mp"), P(DP, "mp"), P("mp"))
    return jax.shard_map(
        shards, mesh=inner_mesh, in_specs=in_specs, out_specs=out_specs, check_vma=False
    )
```

```python
import jax
import jax.numpy as jnp
import numpy as np
from jax import lax
from jax.sharding import Mesh, PartitionSpec as P

TAU = 0.05
LOSS_SCALE = 32.0
EPS = 1e-06
XZ = ("x", "z")
DP = ("x", "z", "c")


def ring_collect(v, name, n):
    if n == 1:
        return v[None]
    me = lax.axis_index(name)
    fwd = [(i, (i + 1) % n) for i in range(n)]
    bwd = [(i, (i - 1) % n) for i in range(n)]
    out = jnp.zeros((n,) + v.shape, v.dtype)
    out = lax.dynamic_update_index_in_dim(out, v, me, 0)
    if n == 2:
        return lax.dynamic_update_index_in_dim(out, lax.ppermute(v, name, fwd), 1 - me, 0)
    n_fwd = n // 2
    n_bwd = (n - 1) // 2
    left = right = v
    for step in range(1, n_fwd + 1):
        if step > n_bwd:
            half = v.shape[0] // 2
            got = jnp.concatenate(
                [lax.ppermute(left[:half], name, fwd), lax.ppermute(right[half:], name, bwd)], axis=0
            )
            out = lax.dynamic_update_index_in_dim(out, got, (me - step) % n, 0)
            break
        left = lax.ppermute(left, name, fwd)
        out = lax.dynamic_update_index_in_dim(out, left, (me - step) % n, 0)
        right = lax.ppermute(right, name, bwd)
        out = lax.dynamic_update_index_in_dim(out, right, (me + step) % n, 0)
    return out


def gather_dp(v):
    gx = ring_collect(v, "x", lax.axis_size("x"))
    gz = ring_collect(gx, "z", lax.axis_size("z"))
    return ring_collect(gz, "c", lax.axis_size("c"))


def ring_reduce(v, name, n, axis):
    if n == 1:
        return v
    me = lax.axis_index(name)
    fwd = [(i, (i + 1) % n) for i in range(n)]
    bwd = [(i, (i - 1) % n) for i in range(n)]

    def block(j):
        return lax.dynamic_index_in_dim(v, j % n, axis, keepdims=False)

    if n == 2:
        return block(me) + lax.ppermute(block(me + 1), name, fwd)
    n_fwd = n // 2
    n_bwd = (n - 1) // 2
    acc_f = block(me + n_fwd)
    for step in range(1, n_fwd + 1):
        acc_f = lax.ppermute(acc_f, name, fwd) + block(me + n_fwd - step)
    total = acc_f
    if n_bwd > 0:
        acc_b = block(me - n_bwd)
        for step in range(1, n_bwd):
            acc_b = lax.ppermute(acc_b, name, bwd) + block(me - n_bwd + step)
        total = total + lax.ppermute(acc_b, name, bwd)
    return total


def split_bf16(v):
    hi = v.astype(jnp.bfloat16)
    lo = (v - hi.astype(jnp.float32)).astype(jnp.bfloat16)
    return jnp.concatenate([hi, lo], axis=0)


def mm(a, b):
    return jnp.dot(a, b, preferred_element_type=jnp.float32)


def shards(attn, resid, w_out, gain, neg_owner, neg_local):
    n_xz = lax.axis_size("x") * lax.axis_size("z")
    n_c = lax.axis_size("c")
    pairs_here = attn.shape[1]
    heads = attn.shape[2]
    feats = resid.shape[2]
    w_rows = w_out.shape[0]
    total = pairs_here * n_xz * n_c

    n_x = lax.axis_size("x")
    n_z = lax.axis_size("z")
    owner_x = neg_owner // (n_z * n_c)
    owner_z = (neg_owner // n_c) % n_z
    owner_c = neg_owner % n_c
    pos = ((owner_c * n_z + owner_z) * n_x + owner_x) * pairs_here + neg_local
    pos_t = pos.T
    pos_all_t = gather_dp(pos).reshape(total, -1).T

    weight_full = gather_dp(w_out).transpose(2, 1, 0, 3, 4).reshape(-1, heads)
    rows_a = attn.reshape(2 * pairs_here, heads)
    proj_part = lax.dot_general(
        rows_a, weight_full, (((1,), (1,)), ((), ())), preferred_element_type=jnp.float32
    )
    proj = lax.psum_scatter(proj_part, "mp", scatter_dimension=1, tiled=True)
    hidden = resid.reshape(2 * pairs_here, feats).astype(jnp.float32) + proj
    normed = hidden * gain
    squares = lax.psum(jnp.sum(normed * normed, axis=1), "mp")
    recip = lax.rsqrt(squares + EPS)[:, None]
    emb = (normed * recip).astype(jnp.bfloat16)
    query = emb[:pairs_here]
    docs = emb[pairs_here:]
    query_f = query.astype(jnp.float32)
    docs_f = docs.astype(jnp.float32)
    emb_all = gather_dp(emb).reshape(n_xz * n_c, 2, pairs_here, feats)
    q_all = emb_all[:, 0].reshape(total, feats)
    e_all = emb_all[:, 1].reshape(total, feats)

    all_scores = lax.dot_general(
        query, e_all, (((1,), (1,)), ((), ())), preferred_element_type=jnp.float32
    )
    neg_part = jnp.take_along_axis(all_scores, pos, axis=1)
    pos_part = jnp.sum(query_f * docs_f, axis=1)
    partial_value = jnp.concatenate([pos_part[:, None], neg_part], axis=1)
    scores = lax.psum(partial_value, "mp") / TAU
    expo = jnp.exp(scores)
    prob = expo / jnp.sum(expo, axis=1, keepdims=True)
    first = (jnp.arange(scores.shape[1]) == 0).astype(jnp.float32)[None, :]
    wts = LOSS_SCALE * (prob - first) / TAU
    wts_neg_t = wts[:, 1:].T
    wts_all_t = gather_dp(wts[:, 1:]).reshape(total, -1).T

    cols = lax.broadcasted_iota(jnp.int32, (1, 1, total), 2)
    coef_q = jnp.sum(jnp.where(pos_t[:, :, None] == cols, wts_neg_t[:, :, None], 0.0), axis=0)
    both = mm(split_bf16(coef_q), e_all)
    grad_query = wts[:, 0:1] * docs_f + both[:pairs_here] + both[pairs_here:]

    me = (lax.axis_index("c") * n_z + lax.axis_index("z")) * n_x + lax.axis_index("x")
    own = me * pairs_here + lax.broadcasted_iota(jnp.int32, (1, pairs_here, 1), 1)
    coef_d = jnp.sum(jnp.where(pos_all_t[:, None, :] == own, wts_all_t[:, None, :], 0.0), axis=0)
    both_d = mm(split_bf16(coef_d), q_all)
    grad_docs = wts[:, 0:1] * query_f + both_d[:pairs_here] + both_d[pairs_here:]

    demb = jnp.concatenate([grad_query, grad_docs], axis=0)
    inner = lax.psum(jnp.sum(normed * demb, axis=1), "mp")[:, None]
    dnorm = recip * demb - recip * recip * recip * normed * inner
    gain_grad = lax.psum(jnp.sum(dnorm * hidden, axis=0), DP)
    dh = (dnorm * gain).astype(jnp.bfloat16)
    dh_full = lax.all_gather(dh, "mp", axis=1, tiled=True)
    attn_grad = mm(dh_full, weight_full).astype(jnp.bfloat16).reshape(attn.shape)
    wg_part = lax.dot_general(
        dh_full, rows_a, (((0,), (0,)), ((), ())), preferred_element_type=jnp.float32
    ).reshape(n_x, n_z, n_c, w_rows, heads)
    wg_xz = ring_reduce(wg_part, "c", n_c, 2)
    wg_x = ring_reduce(wg_xz, "z", n_z, 1)
    weight_grad = ring_reduce(wg_x, "x", n_x, 0)
    return (attn_grad, weight_grad, gain_grad)


def split_mesh(mesh):
    grid = mesh.devices
    n_dp, n_mp = grid.shape
    column = grid[:, 0]
    n_x = len({d.coords[0] for d in column})
    n_c = len({d.core_on_chip for d in column})
    n_z = n_dp // (n_x * n_c)
    return Mesh(grid.reshape(n_x, n_z, n_c, n_mp), ("x", "z", "c", "mp"))


def solution(mesh):
    inner_mesh = split_mesh(mesh)
    in_specs = (
        P(None, DP, "mp"),
        P(None, DP, "mp"),
        P(DP, "mp"),
        P("mp"),
        P(DP, None),
        P(DP, None),
    )
    out_specs = (P(None, DP, "mp"), P(DP, "mp"), P("mp"))
    return jax.shard_map(
        shards, mesh=inner_mesh, in_specs=in_specs, out_specs=out_specs, check_vma=False
    )
```

```python
import jax
import jax.numpy as jnp
import numpy as np
from jax import lax
from jax.sharding import Mesh, PartitionSpec as P

TAU = 0.05
LOSS_SCALE = 32.0
EPS = 1e-06
XZ = ("x", "z")
DP = ("x", "z", "c")


def ring_collect(v, name, n):
    if n == 1:
        return v[None]
    me = lax.axis_index(name)
    fwd = [(i, (i + 1) % n) for i in range(n)]
    bwd = [(i, (i - 1) % n) for i in range(n)]
    out = jnp.zeros((n,) + v.shape, v.dtype)
    out = lax.dynamic_update_index_in_dim(out, v, me, 0)
    if n == 2:
        return lax.dynamic_update_index_in_dim(out, lax.ppermute(v, name, fwd), 1 - me, 0)
    n_fwd = n // 2
    n_bwd = (n - 1) // 2
    left = right = v
    for step in range(1, n_fwd + 1):
        if step > n_bwd:
            half = v.shape[0] // 2
            got = jnp.concatenate(
                [lax.ppermute(left[:half], name, fwd), lax.ppermute(right[half:], name, bwd)], axis=0
            )
            out = lax.dynamic_update_index_in_dim(out, got, (me - step) % n, 0)
            break
        left = lax.ppermute(left, name, fwd)
        out = lax.dynamic_update_index_in_dim(out, left, (me - step) % n, 0)
        right = lax.ppermute(right, name, bwd)
        out = lax.dynamic_update_index_in_dim(out, right, (me + step) % n, 0)
    return out


def gather_dp(v):
    gx = ring_collect(v, "x", lax.axis_size("x"))
    gz = ring_collect(gx, "z", lax.axis_size("z"))
    return ring_collect(gz, "c", lax.axis_size("c"))


def ring_reduce(v, name, n, axis):
    if n == 1:
        return v
    me = lax.axis_index(name)
    fwd = [(i, (i + 1) % n) for i in range(n)]
    bwd = [(i, (i - 1) % n) for i in range(n)]

    def block(j):
        return lax.dynamic_index_in_dim(v, j % n, axis, keepdims=False)

    if n == 2:
        return block(me) + lax.ppermute(block(me + 1), name, fwd)
    n_fwd = n // 2
    n_bwd = (n - 1) // 2
    acc_f = block(me + n_fwd)
    for step in range(1, n_fwd + 1):
        acc_f = lax.ppermute(acc_f, name, fwd) + block(me + n_fwd - step)
    total = acc_f
    if n_bwd > 0:
        acc_b = block(me - n_bwd)
        for step in range(1, n_bwd):
            acc_b = lax.ppermute(acc_b, name, bwd) + block(me - n_bwd + step)
        total = total + lax.ppermute(acc_b, name, bwd)
    return total


def ring_sum(v, name):
    return jnp.sum(ring_collect(v, name, lax.axis_size(name)), axis=0)


def split_bf16(v):
    hi = v.astype(jnp.bfloat16)
    lo = (v - hi.astype(jnp.float32)).astype(jnp.bfloat16)
    return jnp.concatenate([hi, lo], axis=0)


def mm(a, b):
    return jnp.dot(a, b, preferred_element_type=jnp.float32)


def shards(attn, resid, w_out, gain, neg_owner, neg_local):
    n_xz = lax.axis_size("x") * lax.axis_size("z")
    n_c = lax.axis_size("c")
    pairs_here = attn.shape[1]
    heads = attn.shape[2]
    feats = resid.shape[2]
    w_rows = w_out.shape[0]
    total = pairs_here * n_xz * n_c

    n_x = lax.axis_size("x")
    n_z = lax.axis_size("z")
    owner_x = neg_owner // (n_z * n_c)
    owner_z = (neg_owner // n_c) % n_z
    owner_c = neg_owner % n_c
    pos = ((owner_c * n_z + owner_z) * n_x + owner_x) * pairs_here + neg_local
    pos_t = pos.T
    pos_all_t = gather_dp(pos).reshape(total, -1).T

    weight_full = gather_dp(w_out).transpose(2, 1, 0, 3, 4).reshape(-1, heads)
    rows_a = attn.reshape(2 * pairs_here, heads)
    proj_part = lax.dot_general(
        rows_a, weight_full, (((1,), (1,)), ((), ())), preferred_element_type=jnp.float32
    )
    n_mp = lax.axis_size("mp")
    proj = ring_reduce(proj_part.reshape(proj_part.shape[0], n_mp, feats), "mp", n_mp, 1)
    hidden = resid.reshape(2 * pairs_here, feats).astype(jnp.float32) + proj
    normed = hidden * gain
    squares = ring_sum(jnp.sum(normed * normed, axis=1), "mp")
    recip = lax.rsqrt(squares + EPS)[:, None]
    emb = (normed * recip).astype(jnp.bfloat16)
    query = emb[:pairs_here]
    docs = emb[pairs_here:]
    query_f = query.astype(jnp.float32)
    docs_f = docs.astype(jnp.float32)
    emb_all = gather_dp(emb).reshape(n_xz * n_c, 2, pairs_here, feats)
    q_all = emb_all[:, 0].reshape(total, feats)
    e_all = emb_all[:, 1].reshape(total, feats)

    all_scores = lax.dot_general(
        query, e_all, (((1,), (1,)), ((), ())), preferred_element_type=jnp.float32
    )
    neg_part = jnp.take_along_axis(all_scores, pos, axis=1)
    pos_part = jnp.sum(query_f * docs_f, axis=1)
    partial_value = jnp.concatenate([pos_part[:, None], neg_part], axis=1)
    scores = ring_sum(partial_value, "mp") / TAU
    expo = jnp.exp(scores)
    prob = expo / jnp.sum(expo, axis=1, keepdims=True)
    first = (jnp.arange(scores.shape[1]) == 0).astype(jnp.float32)[None, :]
    wts = LOSS_SCALE * (prob - first) / TAU
    wts_neg_t = wts[:, 1:].T
    wts_all_t = gather_dp(wts[:, 1:]).reshape(total, -1).T

    cols = lax.broadcasted_iota(jnp.int32, (1, 1, total), 2)
    coef_q = jnp.sum(jnp.where(pos_t[:, :, None] == cols, wts_neg_t[:, :, None], 0.0), axis=0)
    both = mm(split_bf16(coef_q), e_all)
    grad_query = wts[:, 0:1] * docs_f + both[:pairs_here] + both[pairs_here:]

    me = (lax.axis_index("c") * n_z + lax.axis_index("z")) * n_x + lax.axis_index("x")
    own = me * pairs_here + lax.broadcasted_iota(jnp.int32, (1, pairs_here, 1), 1)
    coef_d = jnp.sum(jnp.where(pos_all_t[:, None, :] == own, wts_all_t[:, None, :], 0.0), axis=0)
    both_d = mm(split_bf16(coef_d), q_all)
    grad_docs = wts[:, 0:1] * query_f + both_d[:pairs_here] + both_d[pairs_here:]

    demb = jnp.concatenate([grad_query, grad_docs], axis=0)
    inner = ring_sum(jnp.sum(normed * demb, axis=1), "mp")[:, None]
    dnorm = recip * demb - recip * recip * recip * normed * inner
    gain_grad = jnp.sum(gather_dp(jnp.sum(dnorm * hidden, axis=0)), axis=(0, 1, 2))
    dh = (dnorm * gain).astype(jnp.bfloat16)
    dh_full = ring_collect(dh, "mp", n_mp).transpose(1, 0, 2).reshape(dh.shape[0], -1)
    attn_grad = mm(dh_full, weight_full).astype(jnp.bfloat16).reshape(attn.shape)
    wg_part = lax.dot_general(
        dh_full, rows_a, (((0,), (0,)), ((), ())), preferred_element_type=jnp.float32
    ).reshape(n_x, n_z, n_c, w_rows, heads)
    wg_xz = ring_reduce(wg_part, "c", n_c, 2)
    wg_x = ring_reduce(wg_xz, "z", n_z, 1)
    weight_grad = ring_reduce(wg_x, "x", n_x, 0)
    return (attn_grad, weight_grad, gain_grad)


def split_mesh(mesh):
    grid = mesh.devices
    n_dp, n_mp = grid.shape
    column = grid[:, 0]
    n_x = len({d.coords[0] for d in column})
    n_c = len({d.core_on_chip for d in column})
    n_z = n_dp // (n_x * n_c)
    return Mesh(grid.reshape(n_x, n_z, n_c, n_mp), ("x", "z", "c", "mp"))


def solution(mesh):
    inner_mesh = split_mesh(mesh)
    in_specs = (
        P(None, DP, "mp"),
        P(None, DP, "mp"),
        P(DP, "mp"),
        P("mp"),
        P(DP, None),
        P(DP, None),
    )
    out_specs = (P(None, DP, "mp"), P(DP, "mp"), P("mp"))
    return jax.shard_map(
        shards, mesh=inner_mesh, in_specs=in_specs, out_specs=out_specs, check_vma=False
    )
```

```python
import jax
import jax.numpy as jnp
import numpy as np
from jax import lax
from jax.sharding import Mesh, PartitionSpec as P

TAU = 0.05
LOSS_SCALE = 32.0
EPS = 1e-06
XZ = ("x", "z")
DP = ("x", "z", "c")


def ring_collect(v, name, n):
    if n == 1:
        return v[None]
    me = lax.axis_index(name)
    fwd = [(i, (i + 1) % n) for i in range(n)]
    bwd = [(i, (i - 1) % n) for i in range(n)]
    out = jnp.zeros((n,) + v.shape, v.dtype)
    out = lax.dynamic_update_index_in_dim(out, v, me, 0)
    if n == 2:
        return lax.dynamic_update_index_in_dim(out, lax.ppermute(v, name, fwd), 1 - me, 0)
    n_fwd = n // 2
    n_bwd = (n - 1) // 2
    left = right = v
    for step in range(1, n_fwd + 1):
        if step > n_bwd and v.size * v.dtype.itemsize < (1 << 19):
            left = lax.ppermute(left, name, fwd)
            out = lax.dynamic_update_index_in_dim(out, left, (me - step) % n, 0)
            break
        if step > n_bwd:
            half = v.shape[0] // 2
            got = jnp.concatenate(
                [lax.ppermute(left[:half], name, fwd), lax.ppermute(right[half:], name, bwd)], axis=0
            )
            out = lax.dynamic_update_index_in_dim(out, got, (me - step) % n, 0)
            break
        left = lax.ppermute(left, name, fwd)
        out = lax.dynamic_update_index_in_dim(out, left, (me - step) % n, 0)
        right = lax.ppermute(right, name, bwd)
        out = lax.dynamic_update_index_in_dim(out, right, (me + step) % n, 0)
    return out


def gather_dp(v):
    gx = ring_collect(v, "x", lax.axis_size("x"))
    gz = ring_collect(gx, "z", lax.axis_size("z"))
    return ring_collect(gz, "c", lax.axis_size("c"))


def ring_reduce(v, name, n, axis):
    if n == 1:
        return v
    me = lax.axis_index(name)
    fwd = [(i, (i + 1) % n) for i in range(n)]
    bwd = [(i, (i - 1) % n) for i in range(n)]

    def block(j):
        return lax.dynamic_index_in_dim(v, j % n, axis, keepdims=False)

    if n == 2:
        return block(me) + lax.ppermute(block(me + 1), name, fwd)
    n_fwd = n // 2
    n_bwd = (n - 1) // 2
    acc_f = block(me + n_fwd)
    for step in range(1, n_fwd + 1):
        acc_f = lax.ppermute(acc_f, name, fwd) + block(me + n_fwd - step)
    total = acc_f
    if n_bwd > 0:
        acc_b = block(me - n_bwd)
        for step in range(1, n_bwd):
            acc_b = lax.ppermute(acc_b, name, bwd) + block(me - n_bwd + step)
        total = total + lax.ppermute(acc_b, name, bwd)
    return total


def ring_sum(v, name):
    return jnp.sum(ring_collect(v, name, lax.axis_size(name)), axis=0)


def split_bf16(v):
    hi = v.astype(jnp.bfloat16)
    lo = (v - hi.astype(jnp.float32)).astype(jnp.bfloat16)
    return jnp.concatenate([hi, lo], axis=0)


def mm(a, b):
    return jnp.dot(a, b, preferred_element_type=jnp.float32)


def shards(attn, resid, w_out, gain, neg_owner, neg_local):
    n_xz = lax.axis_size("x") * lax.axis_size("z")
    n_c = lax.axis_size("c")
    pairs_here = attn.shape[1]
    heads = attn.shape[2]
    feats = resid.shape[2]
    w_rows = w_out.shape[0]
    total = pairs_here * n_xz * n_c

    n_x = lax.axis_size("x")
    n_z = lax.axis_size("z")
    owner_x = neg_owner // (n_z * n_c)
    owner_z = (neg_owner // n_c) % n_z
    owner_c = neg_owner % n_c
    pos = ((owner_c * n_z + owner_z) * n_x + owner_x) * pairs_here + neg_local
    pos_t = pos.T

    weight_full = gather_dp(w_out).transpose(2, 1, 0, 3, 4).reshape(-1, heads)
    rows_a = attn.reshape(2 * pairs_here, heads)
    proj_part = lax.dot_general(
        rows_a, weight_full, (((1,), (1,)), ((), ())), preferred_element_type=jnp.float32
    )
    n_mp = lax.axis_size("mp")
    proj = ring_reduce(proj_part.reshape(proj_part.shape[0], n_mp, feats), "mp", n_mp, 1)
    hidden = resid.reshape(2 * pairs_here, feats).astype(jnp.float32) + proj
    normed = hidden * gain
    squares = ring_sum(jnp.sum(normed * normed, axis=1), "mp")
    recip = lax.rsqrt(squares + EPS)[:, None]
    emb = (normed * recip).astype(jnp.bfloat16)
    query = emb[:pairs_here]
    docs = emb[pairs_here:]
    query_f = query.astype(jnp.float32)
    docs_f = docs.astype(jnp.float32)
    emb_all = gather_dp(emb).reshape(n_xz * n_c, 2, pairs_here, feats)
    q_all = emb_all[:, 0].reshape(total, feats)
    e_all = emb_all[:, 1].reshape(total, feats)

    all_scores = lax.dot_general(
        query, e_all, (((1,), (1,)), ((), ())), preferred_element_type=jnp.float32
    )
    neg_part = jnp.take_along_axis(all_scores, pos, axis=1)
    pos_part = jnp.sum(query_f * docs_f, axis=1)
    partial_value = jnp.concatenate([pos_part[:, None], neg_part], axis=1)
    scores = ring_sum(partial_value, "mp") / TAU
    expo = jnp.exp(scores)
    prob = expo / jnp.sum(expo, axis=1, keepdims=True)
    first = (jnp.arange(scores.shape[1]) == 0).astype(jnp.float32)[None, :]
    wts = LOSS_SCALE * (prob - first) / TAU
    wts_neg_t = wts[:, 1:].T
    neg_count = pos.shape[1]
    packed = jnp.concatenate([wts[:, 1:], pos.astype(jnp.float32)], axis=1)
    packed_all_t = gather_dp(packed).reshape(total, -1).T
    wts_all_t = packed_all_t[:neg_count]
    pos_all_t = packed_all_t[neg_count:].astype(jnp.int32)

    cols = lax.broadcasted_iota(jnp.int32, (1, 1, total), 2)
    coef_q = jnp.sum(jnp.where(pos_t[:, :, None] == cols, wts_neg_t[:, :, None], 0.0), axis=0)
    both = mm(split_bf16(coef_q), e_all)
    grad_query = wts[:, 0:1] * docs_f + both[:pairs_here] + both[pairs_here:]

    me = (lax.axis_index("c") * n_z + lax.axis_index("z")) * n_x + lax.axis_index("x")
    own = me * pairs_here + lax.broadcasted_iota(jnp.int32, (1, pairs_here, 1), 1)
    coef_d = jnp.sum(jnp.where(pos_all_t[:, None, :] == own, wts_all_t[:, None, :], 0.0), axis=0)
    both_d = mm(split_bf16(coef_d), q_all)
    grad_docs = wts[:, 0:1] * query_f + both_d[:pairs_here] + both_d[pairs_here:]

    demb = jnp.concatenate([grad_query, grad_docs], axis=0)
    inner = ring_sum(jnp.sum(normed * demb, axis=1), "mp")[:, None]
    dnorm = recip * demb - recip * recip * recip * normed * inner
    gain_grad = jnp.sum(gather_dp(jnp.sum(dnorm * hidden, axis=0)), axis=(0, 1, 2))
    dh = (dnorm * gain).astype(jnp.bfloat16)
    dh_full = ring_collect(dh, "mp", n_mp).transpose(1, 0, 2).reshape(dh.shape[0], -1)
    attn_grad = mm(dh_full, weight_full).astype(jnp.bfloat16).reshape(attn.shape)
    wg_part = lax.dot_general(
        dh_full, rows_a, (((0,), (0,)), ((), ())), preferred_element_type=jnp.float32
    ).reshape(n_x, n_z, n_c, w_rows, heads)
    wg_xz = ring_reduce(wg_part, "c", n_c, 2)
    wg_x = ring_reduce(wg_xz, "z", n_z, 1)
    weight_grad = ring_reduce(wg_x, "x", n_x, 0)
    return (attn_grad, weight_grad, gain_grad)


def split_mesh(mesh):
    grid = mesh.devices
    n_dp, n_mp = grid.shape
    column = grid[:, 0]
    n_x = len({d.coords[0] for d in column})
    n_c = len({d.core_on_chip for d in column})
    n_z = n_dp // (n_x * n_c)
    return Mesh(grid.reshape(n_x, n_z, n_c, n_mp), ("x", "z", "c", "mp"))


def solution(mesh):
    inner_mesh = split_mesh(mesh)
    in_specs = (
        P(None, DP, "mp"),
        P(None, DP, "mp"),
        P(DP, "mp"),
        P("mp"),
        P(DP, None),
        P(DP, None),
    )
    out_specs = (P(None, DP, "mp"), P(DP, "mp"), P("mp"))
    return jax.shard_map(
        shards, mesh=inner_mesh, in_specs=in_specs, out_specs=out_specs, check_vma=False
    )
```

```python
import jax
import jax.numpy as jnp
import numpy as np
from jax import lax
from jax.sharding import Mesh, PartitionSpec as P

TAU = 0.05
LOSS_SCALE = 32.0
EPS = 1e-06
XZ = ("x", "z")
DP = ("x", "z", "c")


def ring_collect(v, name, n):
    if n == 1:
        return v[None]
    me = lax.axis_index(name)
    fwd = [(i, (i + 1) % n) for i in range(n)]
    bwd = [(i, (i - 1) % n) for i in range(n)]
    out = jnp.zeros((n,) + v.shape, v.dtype)
    out = lax.dynamic_update_index_in_dim(out, v, me, 0)
    if n == 2:
        pair = jnp.stack([v, lax.ppermute(v, name, fwd)])
        return jnp.where(me == 0, pair, pair[::-1])
    n_fwd = n // 2
    n_bwd = (n - 1) // 2
    left = right = v
    for step in range(1, n_fwd + 1):
        if step > n_bwd and v.size * v.dtype.itemsize < (1 << 19):
            left = lax.ppermute(left, name, fwd)
            out = lax.dynamic_update_index_in_dim(out, left, (me - step) % n, 0)
            break
        if step > n_bwd:
            half = v.shape[0] // 2
            got = jnp.concatenate(
                [lax.ppermute(left[:half], name, fwd), lax.ppermute(right[half:], name, bwd)], axis=0
            )
            out = lax.dynamic_update_index_in_dim(out, got, (me - step) % n, 0)
            break
        left = lax.ppermute(left, name, fwd)
        out = lax.dynamic_update_index_in_dim(out, left, (me - step) % n, 0)
        right = lax.ppermute(right, name, bwd)
        out = lax.dynamic_update_index_in_dim(out, right, (me + step) % n, 0)
    return out


def ring_blocks(v, name, n):
    if n == 1:
        return [v]
    fwd = [(i, (i + 1) % n) for i in range(n)]
    bwd = [(i, (i - 1) % n) for i in range(n)]
    if n == 2:
        return [v, lax.ppermute(v, name, fwd)]
    n_fwd = n // 2
    n_bwd = (n - 1) // 2
    blocks = [None] * n
    blocks[0] = v
    left = right = v
    for step in range(1, n_fwd + 1):
        if step > n_bwd and v.size * v.dtype.itemsize >= (1 << 19):
            half = v.shape[0] // 2
            blocks[n - step] = jnp.concatenate(
                [lax.ppermute(left[:half], name, fwd), lax.ppermute(right[half:], name, bwd)], axis=0
            )
            break
        left = lax.ppermute(left, name, fwd)
        blocks[n - step] = left
        if step <= n_bwd:
            right = lax.ppermute(right, name, bwd)
            blocks[step] = right
    return blocks


def gather_rel(v):
    gx = jnp.stack(ring_blocks(v, "x", lax.axis_size("x")))
    gz = jnp.stack(ring_blocks(gx, "z", lax.axis_size("z")))
    return ring_blocks(gz, "c", lax.axis_size("c"))


def gather_dp(v):
    gx = ring_collect(v, "x", lax.axis_size("x"))
    gz = ring_collect(gx, "z", lax.axis_size("z"))
    return ring_collect(gz, "c", lax.axis_size("c"))


def ring_reduce(v, name, n, axis):
    if n == 1:
        return v
    me = lax.axis_index(name)
    fwd = [(i, (i + 1) % n) for i in range(n)]
    bwd = [(i, (i - 1) % n) for i in range(n)]

    def block(j):
        return lax.dynamic_index_in_dim(v, j % n, axis, keepdims=False)

    if n == 2:
        return block(me) + lax.ppermute(block(me + 1), name, fwd)
    n_fwd = n // 2
    n_bwd = (n - 1) // 2
    acc_f = block(me + n_fwd)
    for step in range(1, n_fwd + 1):
        acc_f = lax.ppermute(acc_f, name, fwd) + block(me + n_fwd - step)
    total = acc_f
    if n_bwd > 0:
        acc_b = block(me - n_bwd)
        for step in range(1, n_bwd):
            acc_b = lax.ppermute(acc_b, name, bwd) + block(me - n_bwd + step)
        total = total + lax.ppermute(acc_b, name, bwd)
    return total


def ring_sum(v, name):
    return jnp.sum(ring_collect(v, name, lax.axis_size(name)), axis=0)


def split_bf16(v):
    hi = v.astype(jnp.bfloat16)
    lo = (v - hi.astype(jnp.float32)).astype(jnp.bfloat16)
    return jnp.concatenate([hi, lo], axis=0)


def mm(a, b):
    return jnp.dot(a, b, preferred_element_type=jnp.float32)


def shards(attn, resid, w_out, gain, neg_owner, neg_local):
    n_xz = lax.axis_size("x") * lax.axis_size("z")
    n_c = lax.axis_size("c")
    pairs_here = attn.shape[1]
    heads = attn.shape[2]
    feats = resid.shape[2]
    w_rows = w_out.shape[0]
    total = pairs_here * n_xz * n_c

    n_x = lax.axis_size("x")
    n_z = lax.axis_size("z")
    step_x = (neg_owner // (n_z * n_c) - lax.axis_index("x")) % n_x
    step_z = ((neg_owner // n_c) % n_z - lax.axis_index("z")) % n_z
    step_c = (neg_owner % n_c - lax.axis_index("c")) % n_c
    pos = ((step_c * n_z + step_z) * n_x + step_x) * pairs_here + neg_local
    pos_t = pos.T

    weight_full = gather_dp(w_out).transpose(2, 1, 0, 3, 4).reshape(-1, heads)
    rows_a = attn.reshape(2 * pairs_here, heads)
    proj_part = lax.dot_general(
        rows_a, weight_full, (((1,), (1,)), ((), ())), preferred_element_type=jnp.float32
    )
    n_mp = lax.axis_size("mp")
    proj = ring_reduce(proj_part.reshape(proj_part.shape[0], n_mp, feats), "mp", n_mp, 1)
    hidden = resid.reshape(2 * pairs_here, feats).astype(jnp.float32) + proj
    normed = hidden * gain
    squares = ring_sum(jnp.sum(normed * normed, axis=1), "mp")
    recip = lax.rsqrt(squares + EPS)[:, None]
    emb = (normed * recip).astype(jnp.bfloat16)
    query = emb[:pairs_here]
    docs = emb[pairs_here:]
    query_f = query.astype(jnp.float32)
    docs_f = docs.astype(jnp.float32)
    emb_parts = [b.reshape(n_xz, 2, pairs_here, feats) for b in gather_rel(emb)]
    q_all = jnp.stack([b[:, 0] for b in emb_parts]).reshape(total, feats)
    e_all = jnp.stack([b[:, 1] for b in emb_parts]).reshape(total, feats)

    all_scores = lax.dot_general(
        query, e_all, (((1,), (1,)), ((), ())), preferred_element_type=jnp.float32
    )
    cols = lax.broadcasted_iota(jnp.int32, (1, 1, total), 2)
    neg_part = jnp.sum(jnp.where(pos[:, :, None] == cols, all_scores[:, None, :], 0.0), axis=2)
    pos_part = jnp.sum(query_f * docs_f, axis=1)
    partial_value = jnp.concatenate([pos_part[:, None], neg_part], axis=1)
    scores = ring_sum(partial_value, "mp") / TAU
    expo = jnp.exp(scores)
    prob = expo / jnp.sum(expo, axis=1, keepdims=True)
    first = (jnp.arange(scores.shape[1]) == 0).astype(jnp.float32)[None, :]
    wts = LOSS_SCALE * (prob - first) / TAU
    wts_neg_t = wts[:, 1:].T
    neg_count = pos.shape[1]
    doc_ids = neg_owner * pairs_here + neg_local
    packed = jnp.concatenate([wts[:, 1:], doc_ids.astype(jnp.float32)], axis=1)
    packed_all_t = jnp.stack(gather_rel(packed)).reshape(total, -1).T
    wts_all_t = packed_all_t[:neg_count]
    ids_all_t = packed_all_t[neg_count:].astype(jnp.int32)

    coef_q = jnp.sum(jnp.where(pos_t[:, :, None] == cols, wts_neg_t[:, :, None], 0.0), axis=0)
    both = mm(split_bf16(coef_q), e_all)
    grad_query = wts[:, 0:1] * docs_f + both[:pairs_here] + both[pairs_here:]

    me = (lax.axis_index("x") * n_z + lax.axis_index("z")) * n_c + lax.axis_index("c")
    own = me * pairs_here + lax.broadcasted_iota(jnp.int32, (1, pairs_here, 1), 1)
    coef_d = jnp.sum(jnp.where(ids_all_t[:, None, :] == own, wts_all_t[:, None, :], 0.0), axis=0)
    both_d = mm(split_bf16(coef_d), q_all)
    grad_docs = wts[:, 0:1] * query_f + both_d[:pairs_here] + both_d[pairs_here:]

    demb = jnp.concatenate([grad_query, grad_docs], axis=0)
    inner = ring_sum(jnp.sum(normed * demb, axis=1), "mp")[:, None]
    dnorm = recip * demb - recip * recip * recip * normed * inner
    gain_grad = jnp.sum(gather_dp(jnp.sum(dnorm * hidden, axis=0)), axis=(0, 1, 2))
    dh = (dnorm * gain).astype(jnp.bfloat16)
    dh_full = ring_collect(dh, "mp", n_mp).transpose(1, 0, 2).reshape(dh.shape[0], -1)
    attn_grad = mm(dh_full, weight_full).astype(jnp.bfloat16).reshape(attn.shape)
    wg_part = lax.dot_general(
        dh_full, rows_a, (((0,), (0,)), ((), ())), preferred_element_type=jnp.float32
    ).reshape(n_x, n_z, n_c, w_rows, heads)
    wg_xz = ring_reduce(wg_part, "c", n_c, 2)
    wg_x = ring_reduce(wg_xz, "z", n_z, 1)
    weight_grad = ring_reduce(wg_x, "x", n_x, 0)
    return (attn_grad, weight_grad, gain_grad)


def split_mesh(mesh):
    grid = mesh.devices
    n_dp, n_mp = grid.shape
    column = grid[:, 0]
    n_x = len({d.coords[0] for d in column})
    n_c = len({d.core_on_chip for d in column})
    n_z = n_dp // (n_x * n_c)
    return Mesh(grid.reshape(n_x, n_z, n_c, n_mp), ("x", "z", "c", "mp"))


def solution(mesh):
    inner_mesh = split_mesh(mesh)
    in_specs = (
        P(None, DP, "mp"),
        P(None, DP, "mp"),
        P(DP, "mp"),
        P("mp"),
        P(DP, None),
        P(DP, None),
    )
    out_specs = (P(None, DP, "mp"), P(DP, "mp"), P("mp"))
    return jax.shard_map(
        shards, mesh=inner_mesh, in_specs=in_specs, out_specs=out_specs, check_vma=False
    )
```

```python
import jax
import jax.numpy as jnp
import numpy as np
from jax import lax
from jax.sharding import Mesh, PartitionSpec as P

TAU = 0.05
LOSS_SCALE = 32.0
EPS = 1e-06
XZ = ("x", "z")
DP = ("x", "z", "c")


def ring_collect(v, name, n):
    if n == 1:
        return v[None]
    me = lax.axis_index(name)
    fwd = [(i, (i + 1) % n) for i in range(n)]
    bwd = [(i, (i - 1) % n) for i in range(n)]
    out = jnp.zeros((n,) + v.shape, v.dtype)
    out = lax.dynamic_update_index_in_dim(out, v, me, 0)
    if n == 2:
        pair = jnp.stack([v, lax.ppermute(v, name, fwd)])
        return jnp.where(me == 0, pair, pair[::-1])
    n_fwd = n // 2
    n_bwd = (n - 1) // 2
    left = right = v
    for step in range(1, n_fwd + 1):
        if step > n_bwd and v.size * v.dtype.itemsize < (1 << 19):
            left = lax.ppermute(left, name, fwd)
            out = lax.dynamic_update_index_in_dim(out, left, (me - step) % n, 0)
            break
        if step > n_bwd:
            half = v.shape[0] // 2
            got = jnp.concatenate(
                [lax.ppermute(left[:half], name, fwd), lax.ppermute(right[half:], name, bwd)], axis=0
            )
            out = lax.dynamic_update_index_in_dim(out, got, (me - step) % n, 0)
            break
        left = lax.ppermute(left, name, fwd)
        out = lax.dynamic_update_index_in_dim(out, left, (me - step) % n, 0)
        right = lax.ppermute(right, name, bwd)
        out = lax.dynamic_update_index_in_dim(out, right, (me + step) % n, 0)
    return out


def ring_blocks(v, name, n):
    if n == 1:
        return [v]
    fwd = [(i, (i + 1) % n) for i in range(n)]
    bwd = [(i, (i - 1) % n) for i in range(n)]
    if n == 2:
        return [v, lax.ppermute(v, name, fwd)]
    n_fwd = n // 2
    n_bwd = (n - 1) // 2
    blocks = [None] * n
    blocks[0] = v
    left = right = v
    for step in range(1, n_fwd + 1):
        if step > n_bwd and v.size * v.dtype.itemsize >= (1 << 19):
            half = v.shape[0] // 2
            blocks[n - step] = jnp.concatenate(
                [lax.ppermute(left[:half], name, fwd), lax.ppermute(right[half:], name, bwd)], axis=0
            )
            break
        left = lax.ppermute(left, name, fwd)
        blocks[n - step] = left
        if step <= n_bwd:
            right = lax.ppermute(right, name, bwd)
            blocks[step] = right
    return blocks


def gather_rel(v):
    gx = jnp.stack(ring_blocks(v, "x", lax.axis_size("x")))
    gz = jnp.stack(ring_blocks(gx, "z", lax.axis_size("z")))
    return ring_blocks(gz, "c", lax.axis_size("c"))


def gather_dp(v):
    gx = ring_collect(v, "x", lax.axis_size("x"))
    gz = ring_collect(gx, "z", lax.axis_size("z"))
    return ring_collect(gz, "c", lax.axis_size("c"))


def ring_reduce(v, name, n, axis):
    if n == 1:
        return v
    me = lax.axis_index(name)
    fwd = [(i, (i + 1) % n) for i in range(n)]
    bwd = [(i, (i - 1) % n) for i in range(n)]

    def block(j):
        return lax.dynamic_index_in_dim(v, j % n, axis, keepdims=False)

    if n == 2:
        return block(me) + lax.ppermute(block(me + 1), name, fwd)
    n_fwd = n // 2
    n_bwd = (n - 1) // 2
    acc_f = block(me + n_fwd)
    for step in range(1, n_fwd + 1):
        acc_f = lax.ppermute(acc_f, name, fwd) + block(me + n_fwd - step)
    total = acc_f
    if n_bwd > 0:
        acc_b = block(me - n_bwd)
        for step in range(1, n_bwd):
            acc_b = lax.ppermute(acc_b, name, bwd) + block(me - n_bwd + step)
        total = total + lax.ppermute(acc_b, name, bwd)
    return total


def ring_reduce_carry(v, g, name, n, axis):
    me = lax.axis_index(name)
    fwd = [(i, (i + 1) % n) for i in range(n)]
    bwd = [(i, (i - 1) % n) for i in range(n)]
    cut = v.size // n

    def block(j):
        return lax.dynamic_index_in_dim(v, j % n, axis, keepdims=False)

    def send(acc, part, perm):
        got = lax.ppermute(jnp.concatenate([acc.reshape(-1), part.reshape(-1)]), name, perm)
        return got[:cut].reshape(acc.shape), got[cut:].reshape(part.shape)

    if n == 2:
        acc, other = send(block(me + 1), g, fwd)
        pair = jnp.stack([g, other])
        return block(me) + acc, jnp.where(me == 0, pair, pair[::-1])
    out = jnp.zeros((n,) + g.shape, g.dtype)
    out = lax.dynamic_update_index_in_dim(out, g, me, 0)
    n_fwd = n // 2
    n_bwd = (n - 1) // 2
    acc_f = block(me + n_fwd)
    left = g
    for step in range(1, n_fwd + 1):
        acc, left = send(acc_f, left, fwd)
        acc_f = acc + block(me + n_fwd - step)
        out = lax.dynamic_update_index_in_dim(out, left, (me - step) % n, 0)
    total = acc_f
    acc_b = block(me - n_bwd)
    right = g
    for step in range(1, n_bwd + 1):
        acc, right = send(acc_b, right, bwd)
        out = lax.dynamic_update_index_in_dim(out, right, (me + step) % n, 0)
        if step < n_bwd:
            acc_b = acc + block(me - n_bwd + step)
        else:
            total = total + acc
    return total, out


def ring_sum(v, name):
    return jnp.sum(ring_collect(v, name, lax.axis_size(name)), axis=0)


def split_bf16(v):
    hi = v.astype(jnp.bfloat16)
    lo = (v - hi.astype(jnp.float32)).astype(jnp.bfloat16)
    return jnp.concatenate([hi, lo], axis=0)


def mm(a, b):
    return jnp.dot(a, b, preferred_element_type=jnp.float32)


def shards(attn, resid, w_out, gain, neg_owner, neg_local):
    n_xz = lax.axis_size("x") * lax.axis_size("z")
    n_c = lax.axis_size("c")
    pairs_here = attn.shape[1]
    heads = attn.shape[2]
    feats = resid.shape[2]
    w_rows = w_out.shape[0]
    total = pairs_here * n_xz * n_c

    n_x = lax.axis_size("x")
    n_z = lax.axis_size("z")
    step_x = (neg_owner // (n_z * n_c) - lax.axis_index("x")) % n_x
    step_z = ((neg_owner // n_c) % n_z - lax.axis_index("z")) % n_z
    step_c = (neg_owner % n_c - lax.axis_index("c")) % n_c
    pos = ((step_c * n_z + step_z) * n_x + step_x) * pairs_here + neg_local
    pos_t = pos.T

    weight_full = gather_dp(w_out).transpose(2, 1, 0, 3, 4).reshape(-1, heads)
    rows_a = attn.reshape(2 * pairs_here, heads)
    proj_part = lax.dot_general(
        rows_a, weight_full, (((1,), (1,)), ((), ())), preferred_element_type=jnp.float32
    )
    n_mp = lax.axis_size("mp")
    proj = ring_reduce(proj_part.reshape(proj_part.shape[0], n_mp, feats), "mp", n_mp, 1)
    hidden = resid.reshape(2 * pairs_here, feats).astype(jnp.float32) + proj
    normed = hidden * gain
    squares = ring_sum(jnp.sum(normed * normed, axis=1), "mp")
    recip = lax.rsqrt(squares + EPS)[:, None]
    emb = (normed * recip).astype(jnp.bfloat16)
    query = emb[:pairs_here]
    docs = emb[pairs_here:]
    query_f = query.astype(jnp.float32)
    docs_f = docs.astype(jnp.float32)
    emb_parts = [b.reshape(n_xz, 2, pairs_here, feats) for b in gather_rel(emb)]
    q_all = jnp.stack([b[:, 0] for b in emb_parts]).reshape(total, feats)
    e_all = jnp.stack([b[:, 1] for b in emb_parts]).reshape(total, feats)

    all_scores = lax.dot_general(
        query, e_all, (((1,), (1,)), ((), ())), preferred_element_type=jnp.float32
    )
    cols = lax.broadcasted_iota(jnp.int32, (1, 1, total), 2)
    neg_part = jnp.sum(jnp.where(pos[:, :, None] == cols, all_scores[:, None, :], 0.0), axis=2)
    pos_part = jnp.sum(query_f * docs_f, axis=1)
    partial_value = jnp.concatenate([pos_part[:, None], neg_part], axis=1)
    scores = ring_sum(partial_value, "mp") / TAU
    expo = jnp.exp(scores)
    prob = expo / jnp.sum(expo, axis=1, keepdims=True)
    first = (jnp.arange(scores.shape[1]) == 0).astype(jnp.float32)[None, :]
    wts = LOSS_SCALE * (prob - first) / TAU
    wts_neg_t = wts[:, 1:].T
    neg_count = pos.shape[1]
    doc_ids = neg_owner * pairs_here + neg_local
    packed = jnp.concatenate([wts[:, 1:], doc_ids.astype(jnp.float32)], axis=1)
    packed_all_t = jnp.stack(gather_rel(packed)).reshape(total, -1).T
    wts_all_t = packed_all_t[:neg_count]
    ids_all_t = packed_all_t[neg_count:].astype(jnp.int32)

    coef_q = jnp.sum(jnp.where(pos_t[:, :, None] == cols, wts_neg_t[:, :, None], 0.0), axis=0)
    both = mm(split_bf16(coef_q), e_all)
    grad_query = wts[:, 0:1] * docs_f + both[:pairs_here] + both[pairs_here:]

    me = (lax.axis_index("x") * n_z + lax.axis_index("z")) * n_c + lax.axis_index("c")
    own = me * pairs_here + lax.broadcasted_iota(jnp.int32, (1, pairs_here, 1), 1)
    coef_d = jnp.sum(jnp.where(ids_all_t[:, None, :] == own, wts_all_t[:, None, :], 0.0), axis=0)
    both_d = mm(split_bf16(coef_d), q_all)
    grad_docs = wts[:, 0:1] * query_f + both_d[:pairs_here] + both_d[pairs_here:]

    demb = jnp.concatenate([grad_query, grad_docs], axis=0)
    inner = ring_sum(jnp.sum(normed * demb, axis=1), "mp")[:, None]
    dnorm = recip * demb - recip * recip * recip * normed * inner
    gain_part = jnp.sum(dnorm * hidden, axis=0)
    dh = (dnorm * gain).astype(jnp.bfloat16)
    dh_full = ring_collect(dh, "mp", n_mp).transpose(1, 0, 2).reshape(dh.shape[0], -1)
    attn_grad = mm(dh_full, weight_full).astype(jnp.bfloat16).reshape(attn.shape)
    wg_part = lax.dot_general(
        dh_full, rows_a, (((0,), (0,)), ((), ())), preferred_element_type=jnp.float32
    ).reshape(n_x, n_z, n_c, w_rows, heads)
    wg_xz, gain_c = ring_reduce_carry(wg_part, gain_part, "c", n_c, 2)
    wg_x, gain_zc = ring_reduce_carry(wg_xz, gain_c, "z", n_z, 1)
    weight_grad, gain_xzc = ring_reduce_carry(wg_x, gain_zc, "x", n_x, 0)
    gain_grad = jnp.sum(gain_xzc, axis=(0, 1, 2))
    return (attn_grad, weight_grad, gain_grad)


def split_mesh(mesh):
    grid = mesh.devices
    n_dp, n_mp = grid.shape
    column = grid[:, 0]
    n_x = len({d.coords[0] for d in column})
    n_c = len({d.core_on_chip for d in column})
    n_z = n_dp // (n_x * n_c)
    return Mesh(grid.reshape(n_x, n_z, n_c, n_mp), ("x", "z", "c", "mp"))


def solution(mesh):
    inner_mesh = split_mesh(mesh)
    in_specs = (
        P(None, DP, "mp"),
        P(None, DP, "mp"),
        P(DP, "mp"),
        P("mp"),
        P(DP, None),
        P(DP, None),
    )
    out_specs = (P(None, DP, "mp"), P(DP, "mp"), P("mp"))
    return jax.shard_map(
        shards, mesh=inner_mesh, in_specs=in_specs, out_specs=out_specs, check_vma=False
    )
```

```python
import jax
import jax.numpy as jnp
import numpy as np
from jax import lax
from jax.sharding import Mesh, PartitionSpec as P

TAU = 0.05
LOSS_SCALE = 32.0
EPS = 1e-06
XZ = ("x", "z")
DP = ("x", "z", "c")


def ring_collect(v, name, n):
    if n == 1:
        return v[None]
    me = lax.axis_index(name)
    fwd = [(i, (i + 1) % n) for i in range(n)]
    bwd = [(i, (i - 1) % n) for i in range(n)]
    out = jnp.zeros((n,) + v.shape, v.dtype)
    out = lax.dynamic_update_index_in_dim(out, v, me, 0)
    if n == 2:
        pair = jnp.stack([v, lax.ppermute(v, name, fwd)])
        return jnp.where(me == 0, pair, pair[::-1])
    n_fwd = n // 2
    n_bwd = (n - 1) // 2
    left = right = v
    for step in range(1, n_fwd + 1):
        if step > n_bwd and v.size * v.dtype.itemsize < (1 << 19):
            left = lax.ppermute(left, name, fwd)
            out = lax.dynamic_update_index_in_dim(out, left, (me - step) % n, 0)
            break
        if step > n_bwd:
            half = v.shape[0] // 2
            got = jnp.concatenate(
                [lax.ppermute(left[:half], name, fwd), lax.ppermute(right[half:], name, bwd)], axis=0
            )
            out = lax.dynamic_update_index_in_dim(out, got, (me - step) % n, 0)
            break
        left = lax.ppermute(left, name, fwd)
        out = lax.dynamic_update_index_in_dim(out, left, (me - step) % n, 0)
        right = lax.ppermute(right, name, bwd)
        out = lax.dynamic_update_index_in_dim(out, right, (me + step) % n, 0)
    return out


def ring_blocks(v, name, n):
    if n == 1:
        return [v]
    fwd = [(i, (i + 1) % n) for i in range(n)]
    bwd = [(i, (i - 1) % n) for i in range(n)]
    if n == 2:
        return [v, lax.ppermute(v, name, fwd)]
    n_fwd = n // 2
    n_bwd = (n - 1) // 2
    blocks = [None] * n
    blocks[0] = v
    left = right = v
    for step in range(1, n_fwd + 1):
        if step > n_bwd and v.size * v.dtype.itemsize >= (1 << 19):
            half = v.shape[0] // 2
            blocks[n - step] = jnp.concatenate(
                [lax.ppermute(left[:half], name, fwd), lax.ppermute(right[half:], name, bwd)], axis=0
            )
            break
        left = lax.ppermute(left, name, fwd)
        blocks[n - step] = left
        if step <= n_bwd:
            right = lax.ppermute(right, name, bwd)
            blocks[step] = right
    return blocks


def gather_rel(v, first="x", second="z"):
    g1 = jnp.stack(ring_blocks(v, first, lax.axis_size(first)))
    g2 = jnp.stack(ring_blocks(g1, second, lax.axis_size(second)))
    return ring_blocks(g2, "c", lax.axis_size("c"))


def gather_dp(v):
    gx = ring_collect(v, "x", lax.axis_size("x"))
    gz = ring_collect(gx, "z", lax.axis_size("z"))
    return ring_collect(gz, "c", lax.axis_size("c"))


def ring_reduce(v, name, n, axis):
    if n == 1:
        return v
    me = lax.axis_index(name)
    fwd = [(i, (i + 1) % n) for i in range(n)]
    bwd = [(i, (i - 1) % n) for i in range(n)]

    def block(j):
        return lax.dynamic_index_in_dim(v, j % n, axis, keepdims=False)

    if n == 2:
        return block(me) + lax.ppermute(block(me + 1), name, fwd)
    n_fwd = n // 2
    n_bwd = (n - 1) // 2
    acc_f = block(me + n_fwd)
    for step in range(1, n_fwd + 1):
        acc_f = lax.ppermute(acc_f, name, fwd) + block(me + n_fwd - step)
    total = acc_f
    if n_bwd > 0:
        acc_b = block(me - n_bwd)
        for step in range(1, n_bwd):
            acc_b = lax.ppermute(acc_b, name, bwd) + block(me - n_bwd + step)
        total = total + lax.ppermute(acc_b, name, bwd)
    return total


def ring_sum(v, name):
    return jnp.sum(ring_collect(v, name, lax.axis_size(name)), axis=0)


def split_bf16(v):
    hi = v.astype(jnp.bfloat16)
    lo = (v - hi.astype(jnp.float32)).astype(jnp.bfloat16)
    return jnp.concatenate([hi, lo], axis=0)


def mm(a, b):
    return jnp.dot(a, b, preferred_element_type=jnp.float32)


def shards(attn, resid, w_out, gain, neg_owner, neg_local):
    n_xz = lax.axis_size("x") * lax.axis_size("z")
    n_c = lax.axis_size("c")
    pairs_here = attn.shape[1]
    heads = attn.shape[2]
    feats = resid.shape[2]
    w_rows = w_out.shape[0]
    total = pairs_here * n_xz * n_c

    n_x = lax.axis_size("x")
    n_z = lax.axis_size("z")
    step_x = (neg_owner // (n_z * n_c) - lax.axis_index("x")) % n_x
    step_z = ((neg_owner // n_c) % n_z - lax.axis_index("z")) % n_z
    step_c = (neg_owner % n_c - lax.axis_index("c")) % n_c
    pos = ((step_c * n_x + step_x) * n_z + step_z) * pairs_here + neg_local
    pos_t = pos.T

    weight_full = gather_dp(w_out).transpose(2, 1, 0, 3, 4).reshape(-1, heads)
    rows_a = attn.reshape(2 * pairs_here, heads)
    proj_part = lax.dot_general(
        rows_a, weight_full, (((1,), (1,)), ((), ())), preferred_element_type=jnp.float32
    )
    n_mp = lax.axis_size("mp")
    proj = ring_reduce(proj_part.reshape(proj_part.shape[0], n_mp, feats), "mp", n_mp, 1)
    hidden = resid.reshape(2 * pairs_here, feats).astype(jnp.float32) + proj
    normed = hidden * gain
    squares = ring_sum(jnp.sum(normed * normed, axis=1), "mp")
    recip = lax.rsqrt(squares + EPS)[:, None]
    emb = (normed * recip).astype(jnp.bfloat16)
    query = emb[:pairs_here]
    docs = emb[pairs_here:]
    query_f = query.astype(jnp.float32)
    docs_f = docs.astype(jnp.float32)
    q_all = jnp.stack(gather_rel(query, "x", "z")).reshape(total, feats)
    e_all = jnp.stack(gather_rel(docs, "z", "x")).reshape(total, feats)

    all_scores = lax.dot_general(
        query, e_all, (((1,), (1,)), ((), ())), preferred_element_type=jnp.float32
    )
    cols = lax.broadcasted_iota(jnp.int32, (1, 1, total), 2)
    neg_part = jnp.sum(jnp.where(pos[:, :, None] == cols, all_scores[:, None, :], 0.0), axis=2)
    pos_part = jnp.sum(query_f * docs_f, axis=1)
    partial_value = jnp.concatenate([pos_part[:, None], neg_part], axis=1)
    scores = ring_sum(partial_value, "mp") / TAU
    expo = jnp.exp(scores)
    prob = expo / jnp.sum(expo, axis=1, keepdims=True)
    first = (jnp.arange(scores.shape[1]) == 0).astype(jnp.float32)[None, :]
    wts = LOSS_SCALE * (prob - first) / TAU
    wts_neg_t = wts[:, 1:].T
    neg_count = pos.shape[1]
    doc_ids = neg_owner * pairs_here + neg_local
    packed = jnp.concatenate([wts[:, 1:], doc_ids.astype(jnp.float32)], axis=1)
    packed_all_t = jnp.stack(gather_rel(packed)).reshape(total, -1).T
    wts_all_t = packed_all_t[:neg_count]
    ids_all_t = packed_all_t[neg_count:].astype(jnp.int32)

    coef_q = jnp.sum(jnp.where(pos_t[:, :, None] == cols, wts_neg_t[:, :, None], 0.0), axis=0)
    both = mm(split_bf16(coef_q), e_all)
    grad_query = wts[:, 0:1] * docs_f + both[:pairs_here] + both[pairs_here:]

    me = (lax.axis_index("x") * n_z + lax.axis_index("z")) * n_c + lax.axis_index("c")
    own = me * pairs_here + lax.broadcasted_iota(jnp.int32, (1, pairs_here, 1), 1)
    coef_d = jnp.sum(jnp.where(ids_all_t[:, None, :] == own, wts_all_t[:, None, :], 0.0), axis=0)
    both_d = mm(split_bf16(coef_d), q_all)
    grad_docs = wts[:, 0:1] * query_f + both_d[:pairs_here] + both_d[pairs_here:]

    demb = jnp.concatenate([grad_query, grad_docs], axis=0)
    inner = ring_sum(jnp.sum(normed * demb, axis=1), "mp")[:, None]
    dnorm = recip * demb - recip * recip * recip * normed * inner
    gain_grad = jnp.sum(gather_dp(jnp.sum(dnorm * hidden, axis=0)), axis=(0, 1, 2))
    dh = (dnorm * gain).astype(jnp.bfloat16)
    dh_full = ring_collect(dh, "mp", n_mp).transpose(1, 0, 2).reshape(dh.shape[0], -1)
    attn_grad = mm(dh_full, weight_full).astype(jnp.bfloat16).reshape(attn.shape)
    wg_part = lax.dot_general(
        dh_full, rows_a, (((0,), (0,)), ((), ())), preferred_element_type=jnp.float32
    ).reshape(n_x, n_z, n_c, w_rows, heads)
    wg_xz = ring_reduce(wg_part, "c", n_c, 2)
    wg_x = ring_reduce(wg_xz, "z", n_z, 1)
    weight_grad = ring_reduce(wg_x, "x", n_x, 0)
    return (attn_grad, weight_grad, gain_grad)


def split_mesh(mesh):
    grid = mesh.devices
    n_dp, n_mp = grid.shape
    column = grid[:, 0]
    n_x = len({d.coords[0] for d in column})
    n_c = len({d.core_on_chip for d in column})
    n_z = n_dp // (n_x * n_c)
    return Mesh(grid.reshape(n_x, n_z, n_c, n_mp), ("x", "z", "c", "mp"))


def solution(mesh):
    inner_mesh = split_mesh(mesh)
    in_specs = (
        P(None, DP, "mp"),
        P(None, DP, "mp"),
        P(DP, "mp"),
        P("mp"),
        P(DP, None),
        P(DP, None),
    )
    out_specs = (P(None, DP, "mp"), P(DP, "mp"), P("mp"))
    return jax.shard_map(
        shards, mesh=inner_mesh, in_specs=in_specs, out_specs=out_specs, check_vma=False
    )
```

```python
import jax
import jax.numpy as jnp
import numpy as np
from jax import lax
from jax.sharding import Mesh, PartitionSpec as P

TAU = 0.05
LOSS_SCALE = 32.0
EPS = 1e-06
XZ = ("x", "z")
DP = ("x", "z", "c")


def ring_collect(v, name, n):
    if n == 1:
        return v[None]
    me = lax.axis_index(name)
    fwd = [(i, (i + 1) % n) for i in range(n)]
    bwd = [(i, (i - 1) % n) for i in range(n)]
    out = jnp.zeros((n,) + v.shape, v.dtype)
    out = lax.dynamic_update_index_in_dim(out, v, me, 0)
    if n == 2:
        pair = jnp.stack([v, lax.ppermute(v, name, fwd)])
        return jnp.where(me == 0, pair, pair[::-1])
    n_fwd = n // 2
    n_bwd = (n - 1) // 2
    left = right = v
    for step in range(1, n_fwd + 1):
        if step > n_bwd and v.size * v.dtype.itemsize < (1 << 19):
            left = lax.ppermute(left, name, fwd)
            out = lax.dynamic_update_index_in_dim(out, left, (me - step) % n, 0)
            break
        if step > n_bwd:
            half = v.shape[0] // 2
            got = jnp.concatenate(
                [lax.ppermute(left[:half], name, fwd), lax.ppermute(right[half:], name, bwd)], axis=0
            )
            out = lax.dynamic_update_index_in_dim(out, got, (me - step) % n, 0)
            break
        left = lax.ppermute(left, name, fwd)
        out = lax.dynamic_update_index_in_dim(out, left, (me - step) % n, 0)
        right = lax.ppermute(right, name, bwd)
        out = lax.dynamic_update_index_in_dim(out, right, (me + step) % n, 0)
    return out


def ring_blocks(v, name, n):
    if n == 1:
        return [v]
    fwd = [(i, (i + 1) % n) for i in range(n)]
    bwd = [(i, (i - 1) % n) for i in range(n)]
    if n == 2:
        return [v, lax.ppermute(v, name, fwd)]
    n_fwd = n // 2
    n_bwd = (n - 1) // 2
    blocks = [None] * n
    blocks[0] = v
    left = right = v
    for step in range(1, n_fwd + 1):
        if step > n_bwd and v.size * v.dtype.itemsize >= (1 << 19):
            half = v.shape[0] // 2
            blocks[n - step] = jnp.concatenate(
                [lax.ppermute(left[:half], name, fwd), lax.ppermute(right[half:], name, bwd)], axis=0
            )
            break
        left = lax.ppermute(left, name, fwd)
        blocks[n - step] = left
        if step <= n_bwd:
            right = lax.ppermute(right, name, bwd)
            blocks[step] = right
    return blocks


def gather_rel(v, first="x", second="z"):
    g1 = jnp.stack(ring_blocks(v, first, lax.axis_size(first)))
    g2 = jnp.stack(ring_blocks(g1, second, lax.axis_size(second)))
    return ring_blocks(g2, "c", lax.axis_size("c"))


def gather_dp(v):
    gx = ring_collect(v, "x", lax.axis_size("x"))
    gz = ring_collect(gx, "z", lax.axis_size("z"))
    return ring_collect(gz, "c", lax.axis_size("c"))


def ring_reduce(v, name, n, axis):
    if n == 1:
        return v
    me = lax.axis_index(name)
    fwd = [(i, (i + 1) % n) for i in range(n)]
    bwd = [(i, (i - 1) % n) for i in range(n)]

    def block(j):
        return lax.dynamic_index_in_dim(v, j % n, axis, keepdims=False)

    if n == 2:
        return block(me) + lax.ppermute(block(me + 1), name, fwd)
    n_fwd = n // 2
    n_bwd = (n - 1) // 2
    acc_f = block(me + n_fwd)
    for step in range(1, n_fwd + 1):
        acc_f = lax.ppermute(acc_f, name, fwd) + block(me + n_fwd - step)
    total = acc_f
    if n_bwd > 0:
        acc_b = block(me - n_bwd)
        for step in range(1, n_bwd):
            acc_b = lax.ppermute(acc_b, name, bwd) + block(me - n_bwd + step)
        total = total + lax.ppermute(acc_b, name, bwd)
    return total


def ring_sum(v, name):
    return jnp.sum(ring_collect(v, name, lax.axis_size(name)), axis=0)


def split_bf16(v):
    hi = v.astype(jnp.bfloat16)
    lo = (v - hi.astype(jnp.float32)).astype(jnp.bfloat16)
    return jnp.concatenate([hi, lo], axis=0)


def mm(a, b):
    return jnp.dot(a, b, preferred_element_type=jnp.float32)


def halves_mm(coef, halves):
    width = halves[0].shape[0]
    out = mm(coef[:, :width], halves[0])
    for i in range(1, len(halves)):
        out = out + mm(coef[:, i * width:(i + 1) * width], halves[i])
    return out


def shards(attn, resid, w_out, gain, neg_owner, neg_local):
    n_xz = lax.axis_size("x") * lax.axis_size("z")
    n_c = lax.axis_size("c")
    pairs_here = attn.shape[1]
    heads = attn.shape[2]
    feats = resid.shape[2]
    w_rows = w_out.shape[0]
    total = pairs_here * n_xz * n_c

    n_x = lax.axis_size("x")
    n_z = lax.axis_size("z")
    step_x = (neg_owner // (n_z * n_c) - lax.axis_index("x")) % n_x
    step_z = ((neg_owner // n_c) % n_z - lax.axis_index("z")) % n_z
    step_c = (neg_owner % n_c - lax.axis_index("c")) % n_c
    pos = ((step_c * n_x + step_x) * n_z + step_z) * pairs_here + neg_local
    pos_t = pos.T

    weight_full = gather_dp(w_out).transpose(2, 1, 0, 3, 4).reshape(-1, heads)
    rows_a = attn.reshape(2 * pairs_here, heads)
    proj_part = lax.dot_general(
        rows_a, weight_full, (((1,), (1,)), ((), ())), preferred_element_type=jnp.float32
    )
    n_mp = lax.axis_size("mp")
    proj = ring_reduce(proj_part.reshape(proj_part.shape[0], n_mp, feats), "mp", n_mp, 1)
    hidden = resid.reshape(2 * pairs_here, feats).astype(jnp.float32) + proj
    normed = hidden * gain
    squares = ring_sum(jnp.sum(normed * normed, axis=1), "mp")
    recip = lax.rsqrt(squares + EPS)[:, None]
    emb = (normed * recip).astype(jnp.bfloat16)
    query = emb[:pairs_here]
    docs = emb[pairs_here:]
    query_f = query.astype(jnp.float32)
    docs_f = docs.astype(jnp.float32)
    q_halves = [b.reshape(-1, feats) for b in gather_rel(query, "x", "z")]
    e_halves = [b.reshape(-1, feats) for b in gather_rel(docs, "z", "x")]

    all_scores = jnp.concatenate(
        [
            lax.dot_general(query, b, (((1,), (1,)), ((), ())), preferred_element_type=jnp.float32)
            for b in e_halves
        ],
        axis=1,
    )
    cols = lax.broadcasted_iota(jnp.int32, (1, 1, total), 2)
    neg_part = jnp.sum(jnp.where(pos[:, :, None] == cols, all_scores[:, None, :], 0.0), axis=2)
    pos_part = jnp.sum(query_f * docs_f, axis=1)
    partial_value = jnp.concatenate([pos_part[:, None], neg_part], axis=1)
    scores = ring_sum(partial_value, "mp") / TAU
    expo = jnp.exp(scores)
    prob = expo / jnp.sum(expo, axis=1, keepdims=True)
    first = (jnp.arange(scores.shape[1]) == 0).astype(jnp.float32)[None, :]
    wts = LOSS_SCALE * (prob - first) / TAU
    wts_neg_t = wts[:, 1:].T
    neg_count = pos.shape[1]
    doc_ids = neg_owner * pairs_here + neg_local
    packed = jnp.concatenate([wts[:, 1:], doc_ids.astype(jnp.float32)], axis=1)
    packed_all_t = jnp.stack(gather_rel(packed)).reshape(total, -1).T
    wts_all_t = packed_all_t[:neg_count]
    ids_all_t = packed_all_t[neg_count:].astype(jnp.int32)

    coef_q = jnp.sum(jnp.where(pos_t[:, :, None] == cols, wts_neg_t[:, :, None], 0.0), axis=0)
    both = halves_mm(split_bf16(coef_q), e_halves)
    grad_query = wts[:, 0:1] * docs_f + both[:pairs_here] + both[pairs_here:]

    me = (lax.axis_index("x") * n_z + lax.axis_index("z")) * n_c + lax.axis_index("c")
    own = me * pairs_here + lax.broadcasted_iota(jnp.int32, (1, pairs_here, 1), 1)
    coef_d = jnp.sum(jnp.where(ids_all_t[:, None, :] == own, wts_all_t[:, None, :], 0.0), axis=0)
    both_d = halves_mm(split_bf16(coef_d), q_halves)
    grad_docs = wts[:, 0:1] * query_f + both_d[:pairs_here] + both_d[pairs_here:]

    demb = jnp.concatenate([grad_query, grad_docs], axis=0)
    inner = ring_sum(jnp.sum(normed * demb, axis=1), "mp")[:, None]
    dnorm = recip * demb - recip * recip * recip * normed * inner
    gain_grad = jnp.sum(gather_dp(jnp.sum(dnorm * hidden, axis=0)), axis=(0, 1, 2))
    dh = (dnorm * gain).astype(jnp.bfloat16)
    dh_full = ring_collect(dh, "mp", n_mp).transpose(1, 0, 2).reshape(dh.shape[0], -1)
    attn_grad = mm(dh_full, weight_full).astype(jnp.bfloat16).reshape(attn.shape)
    wg_part = lax.dot_general(
        dh_full, rows_a, (((0,), (0,)), ((), ())), preferred_element_type=jnp.float32
    ).reshape(n_x, n_z, n_c, w_rows, heads)
    wg_xz = ring_reduce(wg_part, "c", n_c, 2)
    wg_x = ring_reduce(wg_xz, "z", n_z, 1)
    weight_grad = ring_reduce(wg_x, "x", n_x, 0)
    return (attn_grad, weight_grad, gain_grad)


def split_mesh(mesh):
    grid = mesh.devices
    n_dp, n_mp = grid.shape
    column = grid[:, 0]
    n_x = len({d.coords[0] for d in column})
    n_c = len({d.core_on_chip for d in column})
    n_z = n_dp // (n_x * n_c)
    return Mesh(grid.reshape(n_x, n_z, n_c, n_mp), ("x", "z", "c", "mp"))


def solution(mesh):
    inner_mesh = split_mesh(mesh)
    in_specs = (
        P(None, DP, "mp"),
        P(None, DP, "mp"),
        P(DP, "mp"),
        P("mp"),
        P(DP, None),
        P(DP, None),
    )
    out_specs = (P(None, DP, "mp"), P(DP, "mp"), P("mp"))
    return jax.shard_map(
        shards, mesh=inner_mesh, in_specs=in_specs, out_specs=out_specs, check_vma=False
    )
```

```python
import jax
import jax.numpy as jnp
import numpy as np
from jax import lax
from jax.sharding import Mesh, PartitionSpec as P

TAU = 0.05
LOSS_SCALE = 32.0
EPS = 1e-06
XZ = ("x", "z")
DP = ("x", "z", "c")


def ring_collect(v, name, n):
    if n == 1:
        return v[None]
    me = lax.axis_index(name)
    fwd = [(i, (i + 1) % n) for i in range(n)]
    bwd = [(i, (i - 1) % n) for i in range(n)]
    out = jnp.zeros((n,) + v.shape, v.dtype)
    out = lax.dynamic_update_index_in_dim(out, v, me, 0)
    if n == 2:
        pair = jnp.stack([v, lax.ppermute(v, name, fwd)])
        return jnp.where(me == 0, pair, pair[::-1])
    n_fwd = n // 2
    n_bwd = (n - 1) // 2
    left = right = v
    for step in range(1, n_fwd + 1):
        if step > n_bwd and v.size * v.dtype.itemsize < (1 << 19):
            left = lax.ppermute(left, name, fwd)
            out = lax.dynamic_update_index_in_dim(out, left, (me - step) % n, 0)
            break
        if step > n_bwd:
            half = v.shape[0] // 2
            got = jnp.concatenate(
                [lax.ppermute(left[:half], name, fwd), lax.ppermute(right[half:], name, bwd)], axis=0
            )
            out = lax.dynamic_update_index_in_dim(out, got, (me - step) % n, 0)
            break
        left = lax.ppermute(left, name, fwd)
        out = lax.dynamic_update_index_in_dim(out, left, (me - step) % n, 0)
        right = lax.ppermute(right, name, bwd)
        out = lax.dynamic_update_index_in_dim(out, right, (me + step) % n, 0)
    return out


def ring_blocks(v, name, n):
    if n == 1:
        return [v]
    fwd = [(i, (i + 1) % n) for i in range(n)]
    bwd = [(i, (i - 1) % n) for i in range(n)]
    if n == 2:
        return [v, lax.ppermute(v, name, fwd)]
    n_fwd = n // 2
    n_bwd = (n - 1) // 2
    blocks = [None] * n
    blocks[0] = v
    left = right = v
    for step in range(1, n_fwd + 1):
        if step > n_bwd and v.size * v.dtype.itemsize >= (1 << 19):
            half = v.shape[0] // 2
            blocks[n - step] = jnp.concatenate(
                [lax.ppermute(left[:half], name, fwd), lax.ppermute(right[half:], name, bwd)], axis=0
            )
            break
        left = lax.ppermute(left, name, fwd)
        blocks[n - step] = left
        if step <= n_bwd:
            right = lax.ppermute(right, name, bwd)
            blocks[step] = right
    return blocks


def gather_rel(v, first="x", second="z"):
    g1 = jnp.stack(ring_blocks(v, first, lax.axis_size(first)))
    g2 = jnp.stack(ring_blocks(g1, second, lax.axis_size(second)))
    return ring_blocks(g2, "c", lax.axis_size("c"))


def gather_dp(v):
    gx = ring_collect(v, "x", lax.axis_size("x"))
    gz = ring_collect(gx, "z", lax.axis_size("z"))
    return ring_collect(gz, "c", lax.axis_size("c"))


def ring_reduce(v, name, n, axis):
    if n == 1:
        return v
    me = lax.axis_index(name)
    fwd = [(i, (i + 1) % n) for i in range(n)]
    bwd = [(i, (i - 1) % n) for i in range(n)]

    def block(j):
        return lax.dynamic_index_in_dim(v, j % n, axis, keepdims=False)

    if n == 2:
        return block(me) + lax.ppermute(block(me + 1), name, fwd)
    n_fwd = n // 2
    n_bwd = (n - 1) // 2
    acc_f = block(me + n_fwd)
    for step in range(1, n_fwd + 1):
        acc_f = lax.ppermute(acc_f, name, fwd) + block(me + n_fwd - step)
    total = acc_f
    if n_bwd > 0:
        acc_b = block(me - n_bwd)
        for step in range(1, n_bwd):
            acc_b = lax.ppermute(acc_b, name, bwd) + block(me - n_bwd + step)
        total = total + lax.ppermute(acc_b, name, bwd)
    return total


def ring_sum(v, name):
    return jnp.sum(ring_collect(v, name, lax.axis_size(name)), axis=0)


def split_bf16(v):
    hi = v.astype(jnp.bfloat16)
    lo = (v - hi.astype(jnp.float32)).astype(jnp.bfloat16)
    return jnp.concatenate([hi, lo], axis=0)


def mm(a, b):
    return jnp.dot(a, b, preferred_element_type=jnp.float32)


def shards(attn, resid, w_out, gain, neg_owner, neg_local):
    n_xz = lax.axis_size("x") * lax.axis_size("z")
    n_c = lax.axis_size("c")
    pairs_here = attn.shape[1]
    heads = attn.shape[2]
    feats = resid.shape[2]
    w_rows = w_out.shape[0]
    total = pairs_here * n_xz * n_c

    n_x = lax.axis_size("x")
    n_z = lax.axis_size("z")
    step_x = (neg_owner // (n_z * n_c) - lax.axis_index("x")) % n_x
    step_z = ((neg_owner // n_c) % n_z - lax.axis_index("z")) % n_z
    step_c = (neg_owner % n_c - lax.axis_index("c")) % n_c
    pos = ((step_c * n_x + step_x) * n_z + step_z) * pairs_here + neg_local
    pos_t = pos.T

    w_z = ring_collect(w_out, "z", n_z)
    w_xz = ring_collect(w_z, "x", n_x)
    weight_full = ring_collect(w_xz, "c", n_c).transpose(1, 2, 0, 3, 4).reshape(-1, heads)
    rows_a = attn.reshape(2 * pairs_here, heads)
    proj_part = lax.dot_general(
        rows_a, weight_full, (((1,), (1,)), ((), ())), preferred_element_type=jnp.float32
    )
    n_mp = lax.axis_size("mp")
    proj = ring_reduce(proj_part.reshape(proj_part.shape[0], n_mp, feats), "mp", n_mp, 1)
    hidden = resid.reshape(2 * pairs_here, feats).astype(jnp.float32) + proj
    normed = hidden * gain
    squares = ring_sum(jnp.sum(normed * normed, axis=1), "mp")
    recip = lax.rsqrt(squares + EPS)[:, None]
    emb = (normed * recip).astype(jnp.bfloat16)
    query = emb[:pairs_here]
    docs = emb[pairs_here:]
    query_f = query.astype(jnp.float32)
    docs_f = docs.astype(jnp.float32)
    q_all = jnp.stack(gather_rel(query, "x", "z")).reshape(total, feats)
    e_all = jnp.stack(gather_rel(docs, "z", "x")).reshape(total, feats)

    all_scores = lax.dot_general(
        query, e_all, (((1,), (1,)), ((), ())), preferred_element_type=jnp.float32
    )
    cols = lax.broadcasted_iota(jnp.int32, (1, 1, total), 2)
    neg_part = jnp.sum(jnp.where(pos[:, :, None] == cols, all_scores[:, None, :], 0.0), axis=2)
    pos_part = jnp.sum(query_f * docs_f, axis=1)
    partial_value = jnp.concatenate([pos_part[:, None], neg_part], axis=1)
    scores = ring_sum(partial_value, "mp") / TAU
    expo = jnp.exp(scores)
    prob = expo / jnp.sum(expo, axis=1, keepdims=True)
    first = (jnp.arange(scores.shape[1]) == 0).astype(jnp.float32)[None, :]
    wts = LOSS_SCALE * (prob - first) / TAU
    wts_neg_t = wts[:, 1:].T
    neg_count = pos.shape[1]
    doc_ids = neg_owner * pairs_here + neg_local
    packed = jnp.concatenate([wts[:, 1:], doc_ids.astype(jnp.float32)], axis=1)
    packed_all_t = jnp.stack(gather_rel(packed)).reshape(total, -1).T
    wts_all_t = packed_all_t[:neg_count]
    ids_all_t = packed_all_t[neg_count:].astype(jnp.int32)

    coef_q = jnp.sum(jnp.where(pos_t[:, :, None] == cols, wts_neg_t[:, :, None], 0.0), axis=0)
    both = mm(split_bf16(coef_q), e_all)
    grad_query = wts[:, 0:1] * docs_f + both[:pairs_here] + both[pairs_here:]

    me = (lax.axis_index("x") * n_z + lax.axis_index("z")) * n_c + lax.axis_index("c")
    own = me * pairs_here + lax.broadcasted_iota(jnp.int32, (1, pairs_here, 1), 1)
    coef_d = jnp.sum(jnp.where(ids_all_t[:, None, :] == own, wts_all_t[:, None, :], 0.0), axis=0)
    both_d = mm(split_bf16(coef_d), q_all)
    grad_docs = wts[:, 0:1] * query_f + both_d[:pairs_here] + both_d[pairs_here:]

    demb = jnp.concatenate([grad_query, grad_docs], axis=0)
    inner = ring_sum(jnp.sum(normed * demb, axis=1), "mp")[:, None]
    dnorm = recip * demb - recip * recip * recip * normed * inner
    gain_grad = jnp.sum(gather_dp(jnp.sum(dnorm * hidden, axis=0)), axis=(0, 1, 2))
    dh = (dnorm * gain).astype(jnp.bfloat16)
    dh_full = ring_collect(dh, "mp", n_mp).transpose(1, 0, 2).reshape(dh.shape[0], -1)
    attn_grad = mm(dh_full, weight_full).astype(jnp.bfloat16).reshape(attn.shape)
    wg_part = lax.dot_general(
        dh_full, rows_a, (((0,), (0,)), ((), ())), preferred_element_type=jnp.float32
    ).reshape(n_x, n_z, n_c, w_rows, heads)
    wg_xz = ring_reduce(wg_part, "c", n_c, 2)
    wg_x = ring_reduce(wg_xz, "z", n_z, 1)
    weight_grad = ring_reduce(wg_x, "x", n_x, 0)
    return (attn_grad, weight_grad, gain_grad)


def split_mesh(mesh):
    grid = mesh.devices
    n_dp, n_mp = grid.shape
    column = grid[:, 0]
    n_x = len({d.coords[0] for d in column})
    n_c = len({d.core_on_chip for d in column})
    n_z = n_dp // (n_x * n_c)
    return Mesh(grid.reshape(n_x, n_z, n_c, n_mp), ("x", "z", "c", "mp"))


def solution(mesh):
    inner_mesh = split_mesh(mesh)
    in_specs = (
        P(None, DP, "mp"),
        P(None, DP, "mp"),
        P(DP, "mp"),
        P("mp"),
        P(DP, None),
        P(DP, None),
    )
    out_specs = (P(None, DP, "mp"), P(DP, "mp"), P("mp"))
    return jax.shard_map(
        shards, mesh=inner_mesh, in_specs=in_specs, out_specs=out_specs, check_vma=False
    )
```

```python
import jax
import jax.numpy as jnp
import numpy as np
from jax import lax
from jax.sharding import Mesh, PartitionSpec as P

TAU = 0.05
LOSS_SCALE = 32.0
EPS = 1e-06
XZ = ("x", "z")
DP = ("x", "z", "c")


def ring_collect(v, name, n):
    if n == 1:
        return v[None]
    me = lax.axis_index(name)
    fwd = [(i, (i + 1) % n) for i in range(n)]
    bwd = [(i, (i - 1) % n) for i in range(n)]
    out = jnp.zeros((n,) + v.shape, v.dtype)
    out = lax.dynamic_update_index_in_dim(out, v, me, 0)
    if n == 2:
        pair = jnp.stack([v, lax.ppermute(v, name, fwd)])
        return jnp.where(me == 0, pair, pair[::-1])
    n_fwd = n // 2
    n_bwd = (n - 1) // 2
    left = right = v
    for step in range(1, n_fwd + 1):
        if step > n_bwd and v.size * v.dtype.itemsize < (1 << 19):
            left = lax.ppermute(left, name, fwd)
            out = lax.dynamic_update_index_in_dim(out, left, (me - step) % n, 0)
            break
        if step > n_bwd:
            half = v.shape[0] // 2
            got = jnp.concatenate(
                [lax.ppermute(left[:half], name, fwd), lax.ppermute(right[half:], name, bwd)], axis=0
            )
            out = lax.dynamic_update_index_in_dim(out, got, (me - step) % n, 0)
            break
        left = lax.ppermute(left, name, fwd)
        out = lax.dynamic_update_index_in_dim(out, left, (me - step) % n, 0)
        right = lax.ppermute(right, name, bwd)
        out = lax.dynamic_update_index_in_dim(out, right, (me + step) % n, 0)
    return out


def ring_blocks(v, name, n):
    if n == 1:
        return [v]
    fwd = [(i, (i + 1) % n) for i in range(n)]
    bwd = [(i, (i - 1) % n) for i in range(n)]
    if n == 2:
        return [v, lax.ppermute(v, name, fwd)]
    n_fwd = n // 2
    n_bwd = (n - 1) // 2
    blocks = [None] * n
    blocks[0] = v
    left = right = v
    for step in range(1, n_fwd + 1):
        if step > n_bwd and v.size * v.dtype.itemsize >= (1 << 19):
            half = v.shape[0] // 2
            blocks[n - step] = jnp.concatenate(
                [lax.ppermute(left[:half], name, fwd), lax.ppermute(right[half:], name, bwd)], axis=0
            )
            break
        left = lax.ppermute(left, name, fwd)
        blocks[n - step] = left
        if step <= n_bwd:
            right = lax.ppermute(right, name, bwd)
            blocks[step] = right
    return blocks


def gather_rel(v, first="x", second="z"):
    g1 = jnp.stack(ring_blocks(v, first, lax.axis_size(first)))
    g2 = jnp.stack(ring_blocks(g1, second, lax.axis_size(second)))
    return ring_blocks(g2, "c", lax.axis_size("c"))


def gather_dp(v):
    gx = ring_collect(v, "x", lax.axis_size("x"))
    gz = ring_collect(gx, "z", lax.axis_size("z"))
    return ring_collect(gz, "c", lax.axis_size("c"))


def ring_reduce(v, name, n, axis, flip=False):
    if n == 1:
        return v
    me = lax.axis_index(name)
    fwd = [(i, (i + 1) % n) for i in range(n)]
    bwd = [(i, (i - 1) % n) for i in range(n)]
    if flip:
        return ring_reduce_mirror(v, name, n, axis, me, fwd, bwd)

    def block(j):
        return lax.dynamic_index_in_dim(v, j % n, axis, keepdims=False)

    if n == 2:
        return block(me) + lax.ppermute(block(me + 1), name, fwd)
    n_fwd = n // 2
    n_bwd = (n - 1) // 2
    acc_f = block(me + n_fwd)
    for step in range(1, n_fwd + 1):
        acc_f = lax.ppermute(acc_f, name, fwd) + block(me + n_fwd - step)
    total = acc_f
    if n_bwd > 0:
        acc_b = block(me - n_bwd)
        for step in range(1, n_bwd):
            acc_b = lax.ppermute(acc_b, name, bwd) + block(me - n_bwd + step)
        total = total + lax.ppermute(acc_b, name, bwd)
    return total


def ring_reduce_mirror(v, name, n, axis, me, fwd, bwd):
    def block(j):
        return lax.dynamic_index_in_dim(v, j % n, axis, keepdims=False)

    n_long = n // 2
    n_short = (n - 1) // 2
    acc_l = block(me - n_long)
    for step in range(1, n_long + 1):
        acc_l = lax.ppermute(acc_l, name, bwd) + block(me - n_long + step)
    total = acc_l
    if n_short > 0:
        acc_s = block(me + n_short)
        for step in range(1, n_short):
            acc_s = lax.ppermute(acc_s, name, fwd) + block(me + n_short - step)
        total = total + lax.ppermute(acc_s, name, fwd)
    return total


def ring_sum(v, name):
    return jnp.sum(ring_collect(v, name, lax.axis_size(name)), axis=0)


def split_bf16(v):
    hi = v.astype(jnp.bfloat16)
    lo = (v - hi.astype(jnp.float32)).astype(jnp.bfloat16)
    return jnp.concatenate([hi, lo], axis=0)


def mm(a, b):
    return jnp.dot(a, b, preferred_element_type=jnp.float32)


def shards(attn, resid, w_out, gain, neg_owner, neg_local):
    n_xz = lax.axis_size("x") * lax.axis_size("z")
    n_c = lax.axis_size("c")
    pairs_here = attn.shape[1]
    heads = attn.shape[2]
    feats = resid.shape[2]
    w_rows = w_out.shape[0]
    total = pairs_here * n_xz * n_c

    n_x = lax.axis_size("x")
    n_z = lax.axis_size("z")
    step_x = (neg_owner // (n_z * n_c) - lax.axis_index("x")) % n_x
    step_z = ((neg_owner // n_c) % n_z - lax.axis_index("z")) % n_z
    step_c = (neg_owner % n_c - lax.axis_index("c")) % n_c
    pos = ((step_c * n_x + step_x) * n_z + step_z) * pairs_here + neg_local
    pos_t = pos.T

    w_z = ring_collect(w_out, "z", n_z)
    w_xz = ring_collect(w_z, "x", n_x)
    weight_full = ring_collect(w_xz, "c", n_c).transpose(1, 2, 0, 3, 4).reshape(-1, heads)
    rows_a = attn.reshape(2 * pairs_here, heads)
    proj_part = lax.dot_general(
        rows_a, weight_full, (((1,), (1,)), ((), ())), preferred_element_type=jnp.float32
    )
    n_mp = lax.axis_size("mp")
    proj_blocks = proj_part.reshape(proj_part.shape[0], n_mp, feats)
    half_f = feats // 2
    proj = jnp.concatenate(
        [
            ring_reduce(proj_blocks[:, :, :half_f], "mp", n_mp, 1),
            ring_reduce(proj_blocks[:, :, half_f:], "mp", n_mp, 1, flip=True),
        ],
        axis=1,
    )
    hidden = resid.reshape(2 * pairs_here, feats).astype(jnp.float32) + proj
    normed = hidden * gain
    squares = ring_sum(jnp.sum(normed * normed, axis=1), "mp")
    recip = lax.rsqrt(squares + EPS)[:, None]
    emb = (normed * recip).astype(jnp.bfloat16)
    query = emb[:pairs_here]
    docs = emb[pairs_here:]
    query_f = query.astype(jnp.float32)
    docs_f = docs.astype(jnp.float32)
    q_all = jnp.stack(gather_rel(query, "x", "z")).reshape(total, feats)
    e_all = jnp.stack(gather_rel(docs, "z", "x")).reshape(total, feats)

    all_scores = lax.dot_general(
        query, e_all, (((1,), (1,)), ((), ())), preferred_element_type=jnp.float32
    )
    cols = lax.broadcasted_iota(jnp.int32, (1, 1, total), 2)
    neg_part = jnp.sum(jnp.where(pos[:, :, None] == cols, all_scores[:, None, :], 0.0), axis=2)
    pos_part = jnp.sum(query_f * docs_f, axis=1)
    partial_value = jnp.concatenate([pos_part[:, None], neg_part], axis=1)
    scores = ring_sum(partial_value, "mp") / TAU
    expo = jnp.exp(scores)
    prob = expo / jnp.sum(expo, axis=1, keepdims=True)
    first = (jnp.arange(scores.shape[1]) == 0).astype(jnp.float32)[None, :]
    wts = LOSS_SCALE * (prob - first) / TAU
    wts_neg_t = wts[:, 1:].T
    neg_count = pos.shape[1]
    doc_ids = neg_owner * pairs_here + neg_local
    packed = jnp.concatenate([wts[:, 1:], doc_ids.astype(jnp.float32)], axis=1)
    packed_all_t = jnp.stack(gather_rel(packed)).reshape(total, -1).T
    wts_all_t = packed_all_t[:neg_count]
    ids_all_t = packed_all_t[neg_count:].astype(jnp.int32)

    coef_q = jnp.sum(jnp.where(pos_t[:, :, None] == cols, wts_neg_t[:, :, None], 0.0), axis=0)
    both = mm(split_bf16(coef_q), e_all)
    grad_query = wts[:, 0:1] * docs_f + both[:pairs_here] + both[pairs_here:]

    me = (lax.axis_index("x") * n_z + lax.axis_index("z")) * n_c + lax.axis_index("c")
    own = me * pairs_here + lax.broadcasted_iota(jnp.int32, (1, pairs_here, 1), 1)
    coef_d = jnp.sum(jnp.where(ids_all_t[:, None, :] == own, wts_all_t[:, None, :], 0.0), axis=0)
    both_d = mm(split_bf16(coef_d), q_all)
    grad_docs = wts[:, 0:1] * query_f + both_d[:pairs_here] + both_d[pairs_here:]

    demb = jnp.concatenate([grad_query, grad_docs], axis=0)
    inner = ring_sum(jnp.sum(normed * demb, axis=1), "mp")[:, None]
    dnorm = recip * demb - recip * recip * recip * normed * inner
    gain_grad = jnp.sum(gather_dp(jnp.sum(dnorm * hidden, axis=0)), axis=(0, 1, 2))
    dh = (dnorm * gain).astype(jnp.bfloat16)
    dh_full = ring_collect(dh, "mp", n_mp).transpose(1, 0, 2).reshape(dh.shape[0], -1)
    attn_grad = mm(dh_full, weight_full).astype(jnp.bfloat16).reshape(attn.shape)
    wg_part = lax.dot_general(
        dh_full, rows_a, (((0,), (0,)), ((), ())), preferred_element_type=jnp.float32
    ).reshape(n_x, n_z, n_c, w_rows, heads)
    wg_xz = ring_reduce(wg_part, "c", n_c, 2)
    wg_x = ring_reduce(wg_xz, "z", n_z, 1)
    weight_grad = ring_reduce(wg_x, "x", n_x, 0)
    return (attn_grad, weight_grad, gain_grad)


def split_mesh(mesh):
    grid = mesh.devices
    n_dp, n_mp = grid.shape
    column = grid[:, 0]
    n_x = len({d.coords[0] for d in column})
    n_c = len({d.core_on_chip for d in column})
    n_z = n_dp // (n_x * n_c)
    return Mesh(grid.reshape(n_x, n_z, n_c, n_mp), ("x", "z", "c", "mp"))


def solution(mesh):
    inner_mesh = split_mesh(mesh)
    in_specs = (
        P(None, DP, "mp"),
        P(None, DP, "mp"),
        P(DP, "mp"),
        P("mp"),
        P(DP, None),
        P(DP, None),
    )
    out_specs = (P(None, DP, "mp"), P(DP, "mp"), P("mp"))
    return jax.shard_map(
        shards, mesh=inner_mesh, in_specs=in_specs, out_specs=out_specs, check_vma=False
    )
```

```python
import jax
import jax.numpy as jnp
import numpy as np
from jax import lax
from jax.sharding import Mesh, PartitionSpec as P

TAU = 0.05
LOSS_SCALE = 32.0
EPS = 1e-06
XZ = ("x", "z")
DP = ("x", "z", "c")


def ring_collect(v, name, n):
    if n == 1:
        return v[None]
    me = lax.axis_index(name)
    fwd = [(i, (i + 1) % n) for i in range(n)]
    bwd = [(i, (i - 1) % n) for i in range(n)]
    out = jnp.zeros((n,) + v.shape, v.dtype)
    out = lax.dynamic_update_index_in_dim(out, v, me, 0)
    if n == 2:
        pair = jnp.stack([v, lax.ppermute(v, name, fwd)])
        return jnp.where(me == 0, pair, pair[::-1])
    n_fwd = n // 2
    n_bwd = (n - 1) // 2
    left = right = v
    for step in range(1, n_fwd + 1):
        if step > n_bwd and v.size * v.dtype.itemsize < (1 << 19):
            left = lax.ppermute(left, name, fwd)
            out = lax.dynamic_update_index_in_dim(out, left, (me - step) % n, 0)
            break
        if step > n_bwd:
            half = v.shape[0] // 2
            got = jnp.concatenate(
                [lax.ppermute(left[:half], name, fwd), lax.ppermute(right[half:], name, bwd)], axis=0
            )
            out = lax.dynamic_update_index_in_dim(out, got, (me - step) % n, 0)
            break
        left = lax.ppermute(left, name, fwd)
        out = lax.dynamic_update_index_in_dim(out, left, (me - step) % n, 0)
        right = lax.ppermute(right, name, bwd)
        out = lax.dynamic_update_index_in_dim(out, right, (me + step) % n, 0)
    return out


def ring_blocks(v, name, n):
    if n == 1:
        return [v]
    fwd = [(i, (i + 1) % n) for i in range(n)]
    bwd = [(i, (i - 1) % n) for i in range(n)]
    if n == 2:
        return [v, lax.ppermute(v, name, fwd)]
    n_fwd = n // 2
    n_bwd = (n - 1) // 2
    blocks = [None] * n
    blocks[0] = v
    left = right = v
    for step in range(1, n_fwd + 1):
        if step > n_bwd and v.size * v.dtype.itemsize >= (1 << 19):
            half = v.shape[0] // 2
            blocks[n - step] = jnp.concatenate(
                [lax.ppermute(left[:half], name, fwd), lax.ppermute(right[half:], name, bwd)], axis=0
            )
            break
        left = lax.ppermute(left, name, fwd)
        blocks[n - step] = left
        if step <= n_bwd:
            right = lax.ppermute(right, name, bwd)
            blocks[step] = right
    return blocks


def gather_rel(v, first="x", second="z"):
    g1 = jnp.stack(ring_blocks(v, first, lax.axis_size(first)))
    g2 = jnp.stack(ring_blocks(g1, second, lax.axis_size(second)))
    return ring_blocks(g2, "c", lax.axis_size("c"))


def gather_dp(v):
    gx = ring_collect(v, "x", lax.axis_size("x"))
    gz = ring_collect(gx, "z", lax.axis_size("z"))
    return ring_collect(gz, "c", lax.axis_size("c"))


def ring_reduce(v, name, n, axis, flip=False):
    if n == 1:
        return v
    me = lax.axis_index(name)
    fwd = [(i, (i + 1) % n) for i in range(n)]
    bwd = [(i, (i - 1) % n) for i in range(n)]
    if flip:
        return ring_reduce_mirror(v, name, n, axis, me, fwd, bwd)

    def block(j):
        return lax.dynamic_index_in_dim(v, j % n, axis, keepdims=False)

    if n == 2:
        return block(me) + lax.ppermute(block(me + 1), name, fwd)
    n_fwd = n // 2
    n_bwd = (n - 1) // 2
    acc_f = block(me + n_fwd)
    for step in range(1, n_fwd + 1):
        acc_f = lax.ppermute(acc_f, name, fwd) + block(me + n_fwd - step)
    total = acc_f
    if n_bwd > 0:
        acc_b = block(me - n_bwd)
        for step in range(1, n_bwd):
            acc_b = lax.ppermute(acc_b, name, bwd) + block(me - n_bwd + step)
        total = total + lax.ppermute(acc_b, name, bwd)
    return total


def ring_reduce_mirror(v, name, n, axis, me, fwd, bwd):
    def block(j):
        return lax.dynamic_index_in_dim(v, j % n, axis, keepdims=False)

    n_long = n // 2
    n_short = (n - 1) // 2
    acc_l = block(me - n_long)
    for step in range(1, n_long + 1):
        acc_l = lax.ppermute(acc_l, name, bwd) + block(me - n_long + step)
    total = acc_l
    if n_short > 0:
        acc_s = block(me + n_short)
        for step in range(1, n_short):
            acc_s = lax.ppermute(acc_s, name, fwd) + block(me + n_short - step)
        total = total + lax.ppermute(acc_s, name, fwd)
    return total


def ring_sum(v, name):
    return jnp.sum(ring_collect(v, name, lax.axis_size(name)), axis=0)


def split_bf16(v):
    hi = v.astype(jnp.bfloat16)
    lo = (v - hi.astype(jnp.float32)).astype(jnp.bfloat16)
    return jnp.concatenate([hi, lo], axis=0)


def mm(a, b):
    return jnp.dot(a, b, preferred_element_type=jnp.float32)


def shards(attn, resid, w_out, gain, neg_owner, neg_local):
    n_xz = lax.axis_size("x") * lax.axis_size("z")
    n_c = lax.axis_size("c")
    pairs_here = attn.shape[1]
    heads = attn.shape[2]
    feats = resid.shape[2]
    w_rows = w_out.shape[0]
    total = pairs_here * n_xz * n_c

    n_x = lax.axis_size("x")
    n_z = lax.axis_size("z")
    step_x = (neg_owner // (n_z * n_c) - lax.axis_index("x")) % n_x
    step_z = ((neg_owner // n_c) % n_z - lax.axis_index("z")) % n_z
    step_c = (neg_owner % n_c - lax.axis_index("c")) % n_c
    pos = ((step_c * n_x + step_x) * n_z + step_z) * pairs_here + neg_local
    pos_t = pos.T

    w_z = ring_collect(w_out, "z", n_z)
    w_xz = ring_collect(w_z, "x", n_x)
    weight_full = ring_collect(w_xz, "c", n_c).transpose(1, 2, 0, 3, 4).reshape(-1, heads)
    rows_a = attn.reshape(2 * pairs_here, heads)
    proj_part = lax.dot_general(
        rows_a, weight_full, (((1,), (1,)), ((), ())), preferred_element_type=jnp.float32
    )
    n_mp = lax.axis_size("mp")
    proj_blocks = proj_part.reshape(proj_part.shape[0], n_mp, feats)
    half_f = feats // 2
    proj = jnp.concatenate(
        [
            ring_reduce(proj_blocks[:, :, :half_f], "mp", n_mp, 1),
            ring_reduce(proj_blocks[:, :, half_f:], "mp", n_mp, 1, flip=True),
        ],
        axis=1,
    )
    hidden = resid.reshape(2 * pairs_here, feats).astype(jnp.float32) + proj
    normed = hidden * gain
    squares = ring_sum(jnp.sum(normed * normed, axis=1), "mp")
    recip = lax.rsqrt(squares + EPS)[:, None]
    emb = (normed * recip).astype(jnp.bfloat16)
    query = emb[:pairs_here]
    docs = emb[pairs_here:]
    query_f = query.astype(jnp.float32)
    docs_f = docs.astype(jnp.float32)
    q_all = jnp.stack(gather_rel(query, "x", "z")).reshape(total, feats)
    e_all = jnp.stack(gather_rel(docs, "z", "x")).reshape(total, feats)

    all_scores = lax.dot_general(
        query, e_all, (((1,), (1,)), ((), ())), preferred_element_type=jnp.float32
    )
    cols = lax.broadcasted_iota(jnp.int32, (1, 1, total), 2)
    neg_part = jnp.sum(jnp.where(pos[:, :, None] == cols, all_scores[:, None, :], 0.0), axis=2)
    pos_part = jnp.sum(query_f * docs_f, axis=1)
    partial_value = jnp.concatenate([pos_part[:, None], neg_part], axis=1)
    scores = ring_sum(partial_value, "mp") / TAU
    expo = jnp.exp(scores)
    prob = expo / jnp.sum(expo, axis=1, keepdims=True)
    first = (jnp.arange(scores.shape[1]) == 0).astype(jnp.float32)[None, :]
    wts = LOSS_SCALE * (prob - first) / TAU
    wts_neg_t = wts[:, 1:].T
    neg_count = pos.shape[1]
    doc_ids = neg_owner * pairs_here + neg_local
    packed = jnp.concatenate([wts[:, 1:], doc_ids.astype(jnp.float32)], axis=1)
    packed_all_t = jnp.stack(gather_rel(packed)).reshape(total, -1).T
    wts_all_t = packed_all_t[:neg_count]
    ids_all_t = packed_all_t[neg_count:].astype(jnp.int32)

    coef_q = jnp.sum(jnp.where(pos_t[:, :, None] == cols, wts_neg_t[:, :, None], 0.0), axis=0)
    both = mm(split_bf16(coef_q), e_all)
    grad_query = wts[:, 0:1] * docs_f + both[:pairs_here] + both[pairs_here:]

    me = (lax.axis_index("x") * n_z + lax.axis_index("z")) * n_c + lax.axis_index("c")
    own = me * pairs_here + lax.broadcasted_iota(jnp.int32, (1, pairs_here, 1), 1)
    coef_d = jnp.sum(jnp.where(ids_all_t[:, None, :] == own, wts_all_t[:, None, :], 0.0), axis=0)
    both_d = mm(split_bf16(coef_d), q_all)
    grad_docs = wts[:, 0:1] * query_f + both_d[:pairs_here] + both_d[pairs_here:]

    demb = jnp.concatenate([grad_query, grad_docs], axis=0)
    inner = ring_sum(jnp.sum(normed * demb, axis=1), "mp")[:, None]
    dnorm = recip * demb - recip * recip * recip * normed * inner
    gain_grad = jnp.sum(gather_dp(jnp.sum(dnorm * hidden, axis=0)), axis=(0, 1, 2))
    dh = (dnorm * gain).astype(jnp.bfloat16)
    dh_full = ring_collect(dh, "mp", n_mp).transpose(1, 0, 2).reshape(dh.shape[0], -1)
    attn_grad = mm(dh_full, weight_full).astype(jnp.bfloat16).reshape(attn.shape)
    wg_part = lax.dot_general(
        dh_full, rows_a, (((0,), (0,)), ((), ())), preferred_element_type=jnp.float32
    ).reshape(n_x, n_z, n_c, w_rows, heads)
    gain_grad, wg_part = lax.optimization_barrier((gain_grad, wg_part))
    wg_xz = ring_reduce(wg_part, "c", n_c, 2)
    wg_x = ring_reduce(wg_xz, "z", n_z, 1)
    weight_grad = ring_reduce(wg_x, "x", n_x, 0)
    return (attn_grad, weight_grad, gain_grad)


def split_mesh(mesh):
    grid = mesh.devices
    n_dp, n_mp = grid.shape
    column = grid[:, 0]
    n_x = len({d.coords[0] for d in column})
    n_c = len({d.core_on_chip for d in column})
    n_z = n_dp // (n_x * n_c)
    return Mesh(grid.reshape(n_x, n_z, n_c, n_mp), ("x", "z", "c", "mp"))


def solution(mesh):
    inner_mesh = split_mesh(mesh)
    in_specs = (
        P(None, DP, "mp"),
        P(None, DP, "mp"),
        P(DP, "mp"),
        P("mp"),
        P(DP, None),
        P(DP, None),
    )
    out_specs = (P(None, DP, "mp"), P(DP, "mp"), P("mp"))
    return jax.shard_map(
        shards, mesh=inner_mesh, in_specs=in_specs, out_specs=out_specs, check_vma=False
    )
```

```python
import jax
import jax.numpy as jnp
import numpy as np
from jax import lax
from jax.sharding import Mesh, PartitionSpec as P

TAU = 0.05
LOSS_SCALE = 32.0
EPS = 1e-06
XZ = ("x", "z")
DP = ("x", "z", "c")


def ring_collect(v, name, n):
    if n == 1:
        return v[None]
    me = lax.axis_index(name)
    fwd = [(i, (i + 1) % n) for i in range(n)]
    bwd = [(i, (i - 1) % n) for i in range(n)]
    out = jnp.zeros((n,) + v.shape, v.dtype)
    out = lax.dynamic_update_index_in_dim(out, v, me, 0)
    if n == 2:
        pair = jnp.stack([v, lax.ppermute(v, name, fwd)])
        return jnp.where(me == 0, pair, pair[::-1])
    n_fwd = n // 2
    n_bwd = (n - 1) // 2
    left = right = v
    for step in range(1, n_fwd + 1):
        if step > n_bwd and v.size * v.dtype.itemsize < (1 << 19):
            left = lax.ppermute(left, name, fwd)
            out = lax.dynamic_update_index_in_dim(out, left, (me - step) % n, 0)
            break
        if step > n_bwd:
            half = v.shape[0] // 2
            got = jnp.concatenate(
                [lax.ppermute(left[:half], name, fwd), lax.ppermute(right[half:], name, bwd)], axis=0
            )
            out = lax.dynamic_update_index_in_dim(out, got, (me - step) % n, 0)
            break
        left = lax.ppermute(left, name, fwd)
        out = lax.dynamic_update_index_in_dim(out, left, (me - step) % n, 0)
        right = lax.ppermute(right, name, bwd)
        out = lax.dynamic_update_index_in_dim(out, right, (me + step) % n, 0)
    return out


def ring_blocks(v, name, n):
    if n == 1:
        return [v]
    fwd = [(i, (i + 1) % n) for i in range(n)]
    bwd = [(i, (i - 1) % n) for i in range(n)]
    if n == 2:
        return [v, lax.ppermute(v, name, fwd)]
    n_fwd = n // 2
    n_bwd = (n - 1) // 2
    blocks = [None] * n
    blocks[0] = v
    left = right = v
    for step in range(1, n_fwd + 1):
        if step > n_bwd and v.size * v.dtype.itemsize >= (1 << 19):
            half = v.shape[0] // 2
            blocks[n - step] = jnp.concatenate(
                [lax.ppermute(left[:half], name, fwd), lax.ppermute(right[half:], name, bwd)], axis=0
            )
            break
        left = lax.ppermute(left, name, fwd)
        blocks[n - step] = left
        if step <= n_bwd:
            right = lax.ppermute(right, name, bwd)
            blocks[step] = right
    return blocks


def gather_rel(v, first="x", second="z"):
    g1 = jnp.stack(ring_blocks(v, first, lax.axis_size(first)))
    g2 = jnp.stack(ring_blocks(g1, second, lax.axis_size(second)))
    return ring_blocks(g2, "c", lax.axis_size("c"))


def gather_dp(v):
    gx = ring_collect(v, "x", lax.axis_size("x"))
    gz = ring_collect(gx, "z", lax.axis_size("z"))
    return ring_collect(gz, "c", lax.axis_size("c"))


def ring_reduce(v, name, n, axis, flip=False):
    if n == 1:
        return v
    me = lax.axis_index(name)
    fwd = [(i, (i + 1) % n) for i in range(n)]
    bwd = [(i, (i - 1) % n) for i in range(n)]
    if flip:
        return ring_reduce_mirror(v, name, n, axis, me, fwd, bwd)

    def block(j):
        return lax.dynamic_index_in_dim(v, j % n, axis, keepdims=False)

    if n == 2:
        return block(me) + lax.ppermute(block(me + 1), name, fwd)
    n_fwd = n // 2
    n_bwd = (n - 1) // 2
    acc_f = block(me + n_fwd)
    for step in range(1, n_fwd + 1):
        acc_f = lax.ppermute(acc_f, name, fwd) + block(me + n_fwd - step)
    total = acc_f
    if n_bwd > 0:
        acc_b = block(me - n_bwd)
        for step in range(1, n_bwd):
            acc_b = lax.ppermute(acc_b, name, bwd) + block(me - n_bwd + step)
        total = total + lax.ppermute(acc_b, name, bwd)
    return total


def ring_reduce_mirror(v, name, n, axis, me, fwd, bwd):
    def block(j):
        return lax.dynamic_index_in_dim(v, j % n, axis, keepdims=False)

    n_long = n // 2
    n_short = (n - 1) // 2
    acc_l = block(me - n_long)
    for step in range(1, n_long + 1):
        acc_l = lax.ppermute(acc_l, name, bwd) + block(me - n_long + step)
    total = acc_l
    if n_short > 0:
        acc_s = block(me + n_short)
        for step in range(1, n_short):
            acc_s = lax.ppermute(acc_s, name, fwd) + block(me + n_short - step)
        total = total + lax.ppermute(acc_s, name, fwd)
    return total


def ring_sum(v, name):
    return jnp.sum(ring_collect(v, name, lax.axis_size(name)), axis=0)


def split_bf16(v):
    hi = v.astype(jnp.bfloat16)
    lo = (v - hi.astype(jnp.float32)).astype(jnp.bfloat16)
    return jnp.concatenate([hi, lo], axis=0)


def mm(a, b):
    return jnp.dot(a, b, preferred_element_type=jnp.float32)


def shards(attn, resid, w_out, gain, neg_owner, neg_local):
    n_xz = lax.axis_size("x") * lax.axis_size("z")
    n_c = lax.axis_size("c")
    pairs_here = attn.shape[1]
    heads = attn.shape[2]
    feats = resid.shape[2]
    w_rows = w_out.shape[0]
    total = pairs_here * n_xz * n_c

    n_x = lax.axis_size("x")
    n_z = lax.axis_size("z")
    step_x = (neg_owner // (n_z * n_c) - lax.axis_index("x")) % n_x
    step_z = ((neg_owner // n_c) % n_z - lax.axis_index("z")) % n_z
    step_c = (neg_owner % n_c - lax.axis_index("c")) % n_c
    pos = ((step_c * n_x + step_x) * n_z + step_z) * pairs_here + neg_local
    pos_t = pos.T

    w_z = ring_collect(w_out, "z", n_z)
    w_xz = ring_collect(w_z, "x", n_x)
    weight_full = ring_collect(w_xz, "c", n_c).transpose(1, 2, 0, 3, 4).reshape(-1, heads)
    rows_a = attn.reshape(2 * pairs_here, heads)
    proj_part = lax.dot_general(
        rows_a, weight_full, (((1,), (1,)), ((), ())), preferred_element_type=jnp.float32
    )
    n_mp = lax.axis_size("mp")
    proj_blocks = proj_part.reshape(proj_part.shape[0], n_mp, feats)
    half_f = feats // 2
    proj = jnp.concatenate(
        [
            ring_reduce(proj_blocks[:, :, :half_f], "mp", n_mp, 1),
            ring_reduce(proj_blocks[:, :, half_f:], "mp", n_mp, 1, flip=True),
        ],
        axis=1,
    )
    hidden = resid.reshape(2 * pairs_here, feats).astype(jnp.float32) + proj
    normed = hidden * gain
    squares = ring_sum(jnp.sum(normed * normed, axis=1), "mp")
    recip = lax.rsqrt(squares + EPS)[:, None]
    emb = (normed * recip).astype(jnp.bfloat16)
    query = emb[:pairs_here]
    docs = emb[pairs_here:]
    query_f = query.astype(jnp.float32)
    docs_f = docs.astype(jnp.float32)
    q_all = jnp.stack(gather_rel(query, "x", "z")).reshape(total, feats)
    e_all = jnp.stack(gather_rel(docs, "z", "x")).reshape(total, feats)

    all_scores = lax.dot_general(
        query, e_all, (((1,), (1,)), ((), ())), preferred_element_type=jnp.float32
    )
    cols = lax.broadcasted_iota(jnp.int32, (1, 1, total), 2)
    neg_part = jnp.sum(jnp.where(pos[:, :, None] == cols, all_scores[:, None, :], 0.0), axis=2)
    pos_part = jnp.sum(query_f * docs_f, axis=1)
    partial_value = jnp.concatenate([pos_part[:, None], neg_part], axis=1)
    scores = ring_sum(partial_value, "mp") / TAU
    expo = jnp.exp(scores)
    prob = expo / jnp.sum(expo, axis=1, keepdims=True)
    first = (jnp.arange(scores.shape[1]) == 0).astype(jnp.float32)[None, :]
    wts = LOSS_SCALE * (prob - first) / TAU
    wts_neg_t = wts[:, 1:].T
    neg_count = pos.shape[1]
    doc_ids = neg_owner * pairs_here + neg_local
    packed = jnp.concatenate([wts[:, 1:], doc_ids.astype(jnp.float32)], axis=1)
    packed_all_t = jnp.stack(gather_rel(packed)).reshape(total, -1).T
    wts_all_t = packed_all_t[:neg_count]
    ids_all_t = packed_all_t[neg_count:].astype(jnp.int32)

    coef_q = jnp.sum(jnp.where(pos_t[:, :, None] == cols, wts_neg_t[:, :, None], 0.0), axis=0)
    both = mm(split_bf16(coef_q), e_all)
    grad_query = wts[:, 0:1] * docs_f + both[:pairs_here] + both[pairs_here:]

    me = (lax.axis_index("x") * n_z + lax.axis_index("z")) * n_c + lax.axis_index("c")
    own = me * pairs_here + lax.broadcasted_iota(jnp.int32, (1, pairs_here, 1), 1)
    coef_d = jnp.sum(jnp.where(ids_all_t[:, None, :] == own, wts_all_t[:, None, :], 0.0), axis=0)
    both_d = mm(split_bf16(coef_d), q_all)
    grad_docs = wts[:, 0:1] * query_f + both_d[:pairs_here] + both_d[pairs_here:]

    demb = jnp.concatenate([grad_query, grad_docs], axis=0)
    inner = ring_sum(jnp.sum(normed * demb, axis=1), "mp")[:, None]
    dnorm = recip * demb - recip * recip * recip * normed * inner
    gain_grad = jnp.sum(gather_dp(jnp.sum(dnorm * hidden, axis=0)), axis=(0, 1, 2))
    dh = (dnorm * gain).astype(jnp.bfloat16)
    dh_full = ring_collect(dh, "mp", n_mp).transpose(1, 0, 2).reshape(dh.shape[0], -1)
    attn_grad = mm(dh_full, weight_full).astype(jnp.bfloat16).reshape(attn.shape)
    wg_part = lax.dot_general(
        dh_full, rows_a, (((0,), (0,)), ((), ())), preferred_element_type=jnp.float32
    ).reshape(n_x, n_z, n_c, w_rows, heads)
    wg_xz = ring_reduce(wg_part, "c", n_c, 2)
    half_h = heads // 2
    wg_x = jnp.concatenate(
        [
            ring_reduce(wg_xz[..., :half_h], "z", n_z, 1),
            ring_reduce(wg_xz[..., half_h:], "z", n_z, 1, flip=True),
        ],
        axis=-1,
    )
    weight_grad = ring_reduce(wg_x, "x", n_x, 0)
    return (attn_grad, weight_grad, gain_grad)


def split_mesh(mesh):
    grid = mesh.devices
    n_dp, n_mp = grid.shape
    column = grid[:, 0]
    n_x = len({d.coords[0] for d in column})
    n_c = len({d.core_on_chip for d in column})
    n_z = n_dp // (n_x * n_c)
    return Mesh(grid.reshape(n_x, n_z, n_c, n_mp), ("x", "z", "c", "mp"))


def solution(mesh):
    inner_mesh = split_mesh(mesh)
    in_specs = (
        P(None, DP, "mp"),
        P(None, DP, "mp"),
        P(DP, "mp"),
        P("mp"),
        P(DP, None),
        P(DP, None),
    )
    out_specs = (P(None, DP, "mp"), P(DP, "mp"), P("mp"))
    return jax.shard_map(
        shards, mesh=inner_mesh, in_specs=in_specs, out_specs=out_specs, check_vma=False
    )
```
